128 devices in a mesh: xb: 16 (over y, z), yb: 8 (over x, core).
Axes of the slice: x: 4, y: 4, z: 4, core: 2. Of those that a mesh axis runs over, the one named last changes fastest.
Arguments:
- initial_guess: float32 [128, 512, 256], P('xb', 'yb'), may hold values from -4 to 4
- right_side: float32 [128, 512, 256], P('xb', 'yb'), may hold values from -8 to 8
- coefficient: float32 [128, 512, 256], P('xb', 'yb'), may hold values from 0.3 to 3
Outputs:
- fine_field: float32 [128, 512, 256], P('xb', 'yb')
- middle_field: float32 [64, 256, 128], P('xb', 'yb')
- lower_field: float32 [32, 128, 64], P('xb', 'yb')
- coarse_field: float32 [16, 64, 32], P('xb', 'yb')
The draws below stay inside these ranges and needn't reach their ends.
All inputs are finite; a program needn't handle non-finite values.
Results may differ from the reference program's by a relative error of at most 0.00002.
Values sent between devices are 32-bit elements; how exact they have to be, the bound alone decides.
No kernel may reach another device: no remote copies, remote signals or barrier semaphores. Data moves between devices by JAX's collectives and lax.ppermute only.
A program may use at most 192 MiB of HBM per device.

```python
import math
import jax
import jax.numpy as jnp

COARSE_ITERS = 8
NX = 128
NY = 512
NZ = 256


def block_levels(stream_key, dims, cuts, low, high):
    factor_of = 1.0
    for dim, blocks in cuts:
        draws = jax.random.uniform(jax.random.fold_in(jax.random.fold_in(stream_key, 6), dim), (blocks,), jnp.float32, low / len(cuts), high / len(cuts))
        factor_of = factor_of * jnp.repeat(jnp.exp(draws), dims[dim] // blocks).reshape((-1,) + (1,) * (len(dims) - 1 - dim))
    return factor_of


def scatter_about(own_key, extent, spread, bound, split=(), held_as=jnp.bfloat16):
    drawn = jax.random.normal(own_key, extent, jnp.float32) * spread
    if len(split) > 0:
        drawn = block_levels(own_key, extent, split, -0.22, 0.18) * drawn
    return jnp.clip(drawn, min=-bound, max=bound).astype(held_as)


def setup_inputs(seed: int = 0) -> dict:
    arg_keys = jax.random.split(jax.random.key(seed), 4)
    return {
        "initial_guess": scatter_about(arg_keys[0], (NX, NY, NZ), 0.5, 4.0, ((0, 16), (1, 8)), jnp.float32),
        "right_side": scatter_about(arg_keys[1], (NX, NY, NZ), 1.0, 8.0, ((0, 16), (1, 8)), jnp.float32),
        "coefficient": jnp.clip(jnp.exp(math.log(3.0) - 2.3025851 * jax.random.uniform(arg_keys[2], (NX, NY, NZ), jnp.float32) ** block_levels(arg_keys[2], (NX, NY, NZ), ((0, 16), (1, 8)), -0.2, 0.2)), 0.3, 3.0),
    }


damping_alpha = 0.05
cheb_theta = 1.15
cheb_delta = 0.85
cheb_sigma = cheb_theta / cheb_delta
cheb_first = 1.0 / cheb_sigma
cheb_second = 1.0 / (2.0 * cheb_sigma - cheb_first)
cheb_carry = cheb_second * cheb_first
cheb_resid = 2.0 * cheb_second / cheb_delta
jacobi_weight = 0.8


def neighbours(padded):
    return [padded[2:, 1:-1, 1:-1], padded[:-2, 1:-1, 1:-1], padded[1:-1, 2:, 1:-1],
            padded[1:-1, :-2, 1:-1], padded[1:-1, 1:-1, 2:], padded[1:-1, 1:-1, :-2]]


def face_weights(padded_coef, scale):
    centre = padded_coef[1:-1, 1:-1, 1:-1]
    weights = [(0.5 * scale) * (centre + other) for other in neighbours(padded_coef)]
    diagonal = damping_alpha + weights[0]
    for other in weights[1:]:
        diagonal = diagonal + other
    return weights, diagonal


def apply_operator(padded, field, weights, diagonal):
    result = diagonal * field
    for weight, other in zip(weights, neighbours(padded)):
        result = result - weight * other
    return result


def smooth_level(start, right_side, coefficient, scale, extend):
    weights, diagonal = face_weights(extend(coefficient), scale)
    if start is None:
        start = jnp.zeros_like(right_side)
        residual = right_side
    else:
        residual = right_side - apply_operator(extend(start), start, weights, diagonal)
    first_step = residual / (cheb_theta * diagonal)
    first = start + first_step
    residual = right_side - apply_operator(extend(first), first, weights, diagonal)
    second_step = cheb_carry * first_step + cheb_resid * residual / diagonal
    second = first + second_step
    residual = right_side - apply_operator(extend(second), second, weights, diagonal)
    return second, residual


def restrict_field(field):
    sx, sy, sz = field.shape
    return field.reshape(sx // 2, 2, sy // 2, 2, sz // 2, 2).sum(axis=(1, 3, 5)) * 0.125


def coarse_solve(right_side, coefficient, scale, extend):
    weights, diagonal = face_weights(extend(coefficient), scale)
    field = jnp.zeros_like(right_side)
    for repeat in range(COARSE_ITERS):
        field = field + jacobi_weight * (right_side - apply_operator(extend(field), field, weights, diagonal)) / diagonal
    leftover = right_side - apply_operator(extend(field), field, weights, diagonal)
    ones_field = jnp.ones_like(right_side)
    image_ones = apply_operator(extend(ones_field), ones_field, weights, diagonal)
    return field + jnp.sum(leftover) / jnp.sum(image_ones)


def extend_all(field):
    return jnp.pad(field, 1)


def reference(initial_guess, right_side, coefficient):
    fine, fine_res = smooth_level(initial_guess, right_side, coefficient, 1.0, extend_all)
    mid_coef = restrict_field(coefficient)
    middle, mid_res = smooth_level(None, restrict_field(fine_res), mid_coef, 0.25, extend_all)
    low_coef = restrict_field(mid_coef)
    lower, low_res = smooth_level(None, restrict_field(mid_res), low_coef, 0.0625, extend_all)
    coarse = coarse_solve(restrict_field(low_res), restrict_field(low_coef), 0.015625, extend_all)
    return fine, middle, lower, coarse
```

```python
import jax
import jax.numpy as jnp
from jax import lax
from jax.sharding import PartitionSpec as P

COARSE_ITERS = 8


damping_alpha = 0.05
cheb_theta = 1.15
cheb_delta = 0.85
cheb_sigma = cheb_theta / cheb_delta
cheb_first = 1.0 / cheb_sigma
cheb_second = 1.0 / (2.0 * cheb_sigma - cheb_first)
cheb_carry = cheb_second * cheb_first
cheb_resid = 2.0 * cheb_second / cheb_delta
jacobi_weight = 0.8


def with_halo(block, sides, width):
    for axis, dim in sides:
        count = lax.axis_size(axis)
        forward = [(i, i + 1) for i in range(count - 1)]
        backward = [(target, source) for source, target in forward]
        low = lax.ppermute(
            lax.slice_in_dim(block, block.shape[dim] - width, None, axis=dim), axis, forward
        )
        high = lax.ppermute(lax.slice_in_dim(block, 0, width, axis=dim), axis, backward)
        block = jnp.concatenate([low, block, high], axis=dim)
    return block


def neighbours(padded):
    return [
        padded[2:, 1:-1, 1:-1],
        padded[:-2, 1:-1, 1:-1],
        padded[1:-1, 2:, 1:-1],
        padded[1:-1, :-2, 1:-1],
        padded[1:-1, 1:-1, 2:],
        padded[1:-1, 1:-1, :-2],
    ]


def face_weights(padded_coef, scale):
    centre = padded_coef[1:-1, 1:-1, 1:-1]
    weights = [0.5 * scale * (centre + other) for other in neighbours(padded_coef)]
    diagonal = damping_alpha + weights[0]
    for other in weights[1:]:
        diagonal = diagonal + other
    return (weights, diagonal)


def apply_operator(padded, field, weights, diagonal):
    result = diagonal * field
    for weight, other in zip(weights, neighbours(padded)):
        result = result - weight * other
    return result


def smooth_level(start, right_side, coefficient, scale, extend, padded_coef=None):
    padded_coef = extend(coefficient)
    weights, diagonal = face_weights(padded_coef, scale)
    if start is None:
        start = jnp.zeros_like(right_side)
        residual = right_side
    else:
        residual = right_side - apply_operator(extend(start), start, weights, diagonal)
    first_step = residual / (cheb_theta * diagonal)
    first = start + first_step
    residual = right_side - apply_operator(extend(first), first, weights, diagonal)
    second_step = cheb_carry * first_step + cheb_resid * residual / diagonal
    second = first + second_step
    residual = right_side - apply_operator(extend(second), second, weights, diagonal)
    return (second, residual)


def pair_matrix(count):
    rows = jnp.arange(count // 2)[:, None]
    cols = jnp.arange(count)[None, :] // 2
    return (rows == cols).astype(jnp.float32)


def restrict_field(field):
    sx, sy, sz = field.shape
    halves = field.reshape(sx // 2, 2, sy, sz)
    summed = halves[:, 0] + halves[:, 1]
    summed = jnp.einsum(
        "xyZ,zZ->xyz", summed, pair_matrix(sz), precision=lax.Precision.HIGHEST
    )
    pairs_y = jnp.broadcast_to(pair_matrix(sy), (sx // 2, sy // 2, sy))
    summed = jnp.einsum(
        "xyY,xYz->xyz", pairs_y, summed, precision=lax.Precision.HIGHEST
    )
    return summed * 0.125


def coarse_solve(right_side, coefficient, scale, extend):
    weights, diagonal = face_weights(extend(coefficient), scale)
    field = jnp.zeros_like(right_side)
    for repeat in range(COARSE_ITERS):
        field = (
            field
            + jacobi_weight
            * (right_side - apply_operator(extend(field), field, weights, diagonal))
            / diagonal
        )
    leftover = right_side - apply_operator(extend(field), field, weights, diagonal)
    ones_field = jnp.ones_like(right_side)
    image_ones = apply_operator(extend(ones_field), ones_field, weights, diagonal)
    return field + jnp.sum(leftover) / jnp.sum(image_ones)


def extend_all(field):
    return jnp.pad(field, 1)


def extend_local(field):
    padded = with_halo(field, (("xb", 0), ("yb", 1)), 1)
    return jnp.pad(padded, ((0, 0), (0, 0), (1, 1)))


def collect_grid(right_side, coefficient):
    sx, sy, sz = right_side.shape
    count_x = lax.axis_size("xb")
    count_y = lax.axis_size("yb")
    flat = (
        lax.all_gather(right_side.reshape(1, -1), ("xb", "yb"), axis=0, tiled=True),
        lax.all_gather(coefficient.reshape(1, -1), ("xb", "yb"), axis=0, tiled=True),
    )
    return tuple(
        (
            piece.reshape(count_x, count_y, sx, sy, sz)
            .transpose(0, 2, 1, 3, 4)
            .reshape(count_x * sx, count_y * sy, sz)
            for piece in flat
        )
    )


def own_block(whole, shape):
    start_x = lax.axis_index("xb") * shape[0]
    start_y = lax.axis_index("yb") * shape[1]
    return lax.dynamic_slice(whole, (start_x, start_y, jnp.int32(0)), shape)


def per_device(initial_guess, right_side, coefficient):
    fine, fine_res = smooth_level(initial_guess, right_side, coefficient, 1.0, extend_local, None)
    mid_coef = restrict_field(coefficient)
    middle, mid_res = smooth_level(
        None, restrict_field(fine_res), mid_coef, 0.25, extend_local, None
    )
    low_coef = restrict_field(mid_coef)
    low_rhs = restrict_field(mid_res)
    lower, low_res = smooth_level(None, low_rhs, low_coef, 0.0625, extend_local, None)
    coarse_rhs, coarse_coef = collect_grid(restrict_field(low_res), restrict_field(low_coef))
    coarse_whole = coarse_solve(coarse_rhs, coarse_coef, 0.015625, extend_all)
    sx, sy, sz = right_side.shape
    coarse = own_block(coarse_whole, (sx // 8, sy // 8, sz // 8))
    return (fine, middle, lower, coarse)


def solution(mesh):
    placed = (P("xb", "yb", None), P("xb", "yb", None), P("xb", "yb", None))
    return jax.shard_map(
        per_device,
        mesh=mesh,
        in_specs=placed,
        out_specs=(
            P("xb", "yb", None),
            P("xb", "yb", None),
            P("xb", "yb", None),
            P("xb", "yb", None),
        ),
        check_vma=False,
    )
```

```python
import jax
import jax.numpy as jnp
from jax import lax
from jax.sharding import PartitionSpec as P

COARSE_ITERS = 8


damping_alpha = 0.05
cheb_theta = 1.15
cheb_delta = 0.85
cheb_sigma = cheb_theta / cheb_delta
cheb_first = 1.0 / cheb_sigma
cheb_second = 1.0 / (2.0 * cheb_sigma - cheb_first)
cheb_carry = cheb_second * cheb_first
cheb_resid = 2.0 * cheb_second / cheb_delta
jacobi_weight = 0.8


def exchange(items, axis, dim):
    count = lax.axis_size(axis)
    low = [[] for _ in items]
    high = [[] for _ in items]
    reach = max(-(-width // block.shape[dim]) for block, width in items)
    for hop in range(1, reach + 1):
        for sign in (1, -1):
            pieces = []
            for block, width in items:
                size = block.shape[dim]
                rows = min(size, width - (hop - 1) * size)
                if rows <= 0:
                    pieces.append(None)
                elif sign == 1:
                    pieces.append(lax.slice_in_dim(block, size - rows, size, axis=dim))
                else:
                    pieces.append(lax.slice_in_dim(block, 0, rows, axis=dim))
            flat = jnp.concatenate([p.reshape(-1) for p in pieces if p is not None])
            if sign == 1:
                pairs = [(i, i + hop) for i in range(count - hop)]
            else:
                pairs = [(i + hop, i) for i in range(count - hop)]
            got = lax.ppermute(flat, axis, pairs)
            offset = 0
            for index, piece in enumerate(pieces):
                if piece is None:
                    continue
                part = got[offset : offset + piece.size].reshape(piece.shape)
                offset += piece.size
                if sign == 1:
                    low[index].insert(0, part)
                else:
                    high[index].append(part)
    return [
        jnp.concatenate(low[i] + [block] + high[i], axis=dim)
        for i, (block, width) in enumerate(items)
    ]


def exchange_xy(items):
    widths = [width for _, width in items]
    extended = exchange(items, "xb", 0)
    return exchange(list(zip(extended, widths)), "yb", 1)


def inside_mask(shape, halo):
    sx, sy, _ = shape
    gx = lax.axis_index("xb") * sx - halo + jnp.arange(sx + 2 * halo)
    gy = lax.axis_index("yb") * sy - halo + jnp.arange(sy + 2 * halo)
    in_x = (gx >= 0) & (gx < sx * lax.axis_size("xb"))
    in_y = (gy >= 0) & (gy < sy * lax.axis_size("yb"))
    return in_x[:, None, None] & in_y[None, :, None]


def pad_z(box):
    return jnp.pad(box, ((0, 0), (0, 0), (1, 1)))


def trim(box):
    return box[1:-1, 1:-1, :]


def neighbours(padded):
    return [
        padded[2:, 1:-1, 1:-1],
        padded[:-2, 1:-1, 1:-1],
        padded[1:-1, 2:, 1:-1],
        padded[1:-1, :-2, 1:-1],
        padded[1:-1, 1:-1, 2:],
        padded[1:-1, 1:-1, :-2],
    ]


def face_weights(padded_coef, scale):
    centre = padded_coef[1:-1, 1:-1, 1:-1]
    weights = [0.5 * scale * (centre + other) for other in neighbours(padded_coef)]
    diagonal = damping_alpha + weights[0]
    for other in weights[1:]:
        diagonal = diagonal + other
    return (weights, diagonal)


def apply_operator(padded, field, weights, diagonal):
    result = diagonal * field
    for weight, other in zip(weights, neighbours(padded)):
        result = result - weight * other
    return result


def smooth_level(start, right_side, coefficient, scale, extend):
    weights, diagonal = face_weights(extend(coefficient), scale)
    if start is None:
        start = jnp.zeros_like(right_side)
        residual = right_side
    else:
        residual = right_side - apply_operator(extend(start), start, weights, diagonal)
    first_step = residual / (cheb_theta * diagonal)
    first = start + first_step
    residual = right_side - apply_operator(extend(first), first, weights, diagonal)
    second_step = cheb_carry * first_step + cheb_resid * residual / diagonal
    second = first + second_step
    residual = right_side - apply_operator(extend(second), second, weights, diagonal)
    return (second, residual)


def pair_matrix(count):
    rows = jnp.arange(count // 2)[:, None]
    cols = jnp.arange(count)[None, :] // 2
    return (rows == cols).astype(jnp.float32)


def restrict_field(field):
    sx, sy, sz = field.shape
    halves = field.reshape(sx // 2, 2, sy, sz)
    summed = halves[:, 0] + halves[:, 1]
    summed = jnp.einsum(
        "xyZ,zZ->xyz", summed, pair_matrix(sz), precision=lax.Precision.HIGHEST
    )
    pairs_y = jnp.broadcast_to(pair_matrix(sy), (sx // 2, sy // 2, sy))
    summed = jnp.einsum(
        "xyY,xYz->xyz", pairs_y, summed, precision=lax.Precision.HIGHEST
    )
    return summed * 0.125


def coarse_solve(right_side, coefficient, scale, extend):
    weights, diagonal = face_weights(extend(coefficient), scale)
    field = jnp.zeros_like(right_side)
    for repeat in range(COARSE_ITERS):
        field = (
            field
            + jacobi_weight
            * (right_side - apply_operator(extend(field), field, weights, diagonal))
            / diagonal
        )
    leftover = right_side - apply_operator(extend(field), field, weights, diagonal)
    ones_field = jnp.ones_like(right_side)
    image_ones = apply_operator(extend(ones_field), ones_field, weights, diagonal)
    return field + jnp.sum(leftover) / jnp.sum(image_ones)


def extend_all(field):
    return jnp.pad(field, 1)


def smooth_box(start, right_side, coefficient, scale, shape):
    weights, diagonal = face_weights(pad_z(coefficient), scale)
    if start is None:
        start = jnp.zeros_like(right_side)
        residual = right_side
    else:
        residual = right_side - apply_operator(pad_z(start), trim(start), weights, diagonal)
        start = trim(start)
    first_step = residual / (cheb_theta * diagonal)
    first = jnp.where(inside_mask(shape, 2), start + first_step, 0.0)
    weights = [trim(w) for w in weights]
    diagonal = trim(diagonal)
    right_side = trim(right_side)
    residual = right_side - apply_operator(pad_z(first), trim(first), weights, diagonal)
    second_step = cheb_carry * trim(first_step) + cheb_resid * residual / diagonal
    second = jnp.where(inside_mask(shape, 1), trim(first) + second_step, 0.0)
    weights = [trim(w) for w in weights]
    diagonal = trim(diagonal)
    residual = trim(right_side) - apply_operator(pad_z(second), trim(second), weights, diagonal)
    return (trim(second), residual)


def collect_grid(right_side, coefficient):
    sx, sy, sz = right_side.shape
    count_x = lax.axis_size("xb")
    count_y = lax.axis_size("yb")
    flat = jnp.concatenate([right_side.reshape(1, -1), coefficient.reshape(1, -1)], axis=1)
    both = lax.all_gather(flat, ("xb", "yb"), axis=0, tiled=True)
    size = sx * sy * sz
    return tuple(
        (
            piece.reshape(count_x, count_y, sx, sy, sz)
            .transpose(0, 2, 1, 3, 4)
            .reshape(count_x * sx, count_y * sy, sz)
            for piece in (both[:, :size], both[:, size:])
        )
    )


def own_block(whole, shape):
    start_x = lax.axis_index("xb") * shape[0]
    start_y = lax.axis_index("yb") * shape[1]
    return lax.dynamic_slice(whole, (start_x, start_y, jnp.int32(0)), shape)


def per_device(initial_guess, right_side, coefficient):
    mid_coef = restrict_field(coefficient)
    low_coef = restrict_field(mid_coef)
    guess_b, rhs_b, coef_b, mid_coef_b, low_coef_b = exchange_xy(
        [(initial_guess, 3), (right_side, 2), (coefficient, 3), (mid_coef, 3), (low_coef, 3)]
    )
    fine, fine_res = smooth_box(guess_b, rhs_b, coef_b, 1.0, right_side.shape)
    mid_rhs = restrict_field(fine_res)
    (mid_rhs_b,) = exchange_xy([(mid_rhs, 2)])
    middle, mid_res = smooth_box(None, mid_rhs_b, mid_coef_b, 0.25, mid_rhs.shape)
    low_rhs = restrict_field(mid_res)
    (low_rhs_b,) = exchange_xy([(low_rhs, 2)])
    lower, low_res = smooth_box(None, low_rhs_b, low_coef_b, 0.0625, low_rhs.shape)
    coarse_rhs, coarse_coef = collect_grid(restrict_field(low_res), restrict_field(low_coef))
    coarse_whole = coarse_solve(coarse_rhs, coarse_coef, 0.015625, extend_all)
    sx, sy, sz = right_side.shape
    coarse = own_block(coarse_whole, (sx // 8, sy // 8, sz // 8))
    return (fine, middle, lower, coarse)


def solution(mesh):
    placed = (P("xb", "yb", None), P("xb", "yb", None), P("xb", "yb", None))
    return jax.shard_map(
        per_device,
        mesh=mesh,
        in_specs=placed,
        out_specs=(
            P("xb", "yb", None),
            P("xb", "yb", None),
            P("xb", "yb", None),
            P("xb", "yb", None),
        ),
        check_vma=False,
    )
```

```python
import jax
import jax.numpy as jnp
from jax import lax
from jax.sharding import PartitionSpec as P

COARSE_ITERS = 8


damping_alpha = 0.05
cheb_theta = 1.15
cheb_delta = 0.85
cheb_sigma = cheb_theta / cheb_delta
cheb_first = 1.0 / cheb_sigma
cheb_second = 1.0 / (2.0 * cheb_sigma - cheb_first)
cheb_carry = cheb_second * cheb_first
cheb_resid = 2.0 * cheb_second / cheb_delta
jacobi_weight = 0.8


def exchange(items, axis, dim, forwards=()):
    count = lax.axis_size(axis)
    low = [[] for _ in items]
    high = [[] for _ in items]
    reach = max(-(-width // block.shape[dim]) for block, width in items)
    boxes = [box for box, _, _ in forwards]
    for hop in range(1, reach + 1):
        for sign in (1, -1):
            pieces = []
            for block, width in items:
                size = block.shape[dim]
                rows = min(size, width - (hop - 1) * size)
                if rows <= 0:
                    pieces.append(None)
                elif sign == 1:
                    pieces.append(lax.slice_in_dim(block, size - rows, size, axis=dim))
                else:
                    pieces.append(lax.slice_in_dim(block, 0, rows, axis=dim))
            if hop == 1:
                for box, rows_low, rows_high in forwards:
                    rows = rows_low if sign == 1 else rows_high
                    pieces.append(lax.slice_in_dim(box, rows[0], rows[1], axis=dim))
            flat = jnp.concatenate([p.reshape(-1) for p in pieces if p is not None])
            if sign == 1:
                pairs = [(i, i + hop) for i in range(count - hop)]
            else:
                pairs = [(i + hop, i) for i in range(count - hop)]
            got = lax.ppermute(flat, axis, pairs)
            offset = 0
            parts = []
            for piece in pieces:
                if piece is None:
                    parts.append(None)
                    continue
                parts.append(got[offset : offset + piece.size].reshape(piece.shape))
                offset += piece.size
            for index in range(len(items)):
                if parts[index] is None:
                    continue
                if sign == 1:
                    low[index].insert(0, parts[index])
                else:
                    high[index].append(parts[index])
            if hop == 1:
                for index, part in enumerate(parts[len(items) :]):
                    if sign == 1:
                        boxes[index] = jnp.concatenate([part, boxes[index]], axis=dim)
                    else:
                        boxes[index] = jnp.concatenate([boxes[index], part], axis=dim)
    extended = [
        jnp.concatenate(low[i] + [block] + high[i], axis=dim)
        for i, (block, width) in enumerate(items)
    ]
    return extended, boxes


def exchange_xy(items, forwards=()):
    widths = [item[-1] for item in items]
    extended, boxes = exchange([item[:2] for item in items], "xb", 0, forwards)
    extended, _ = exchange(list(zip(extended, widths)), "yb", 1)
    return extended, boxes


def inside_mask(shape, halo):
    sx, sy, _ = shape
    gx = lax.axis_index("xb") * sx - halo + jnp.arange(sx + 2 * halo)
    gy = lax.axis_index("yb") * sy - halo + jnp.arange(sy + 2 * halo)
    in_x = (gx >= 0) & (gx < sx * lax.axis_size("xb"))
    in_y = (gy >= 0) & (gy < sy * lax.axis_size("yb"))
    return in_x[:, None, None] & in_y[None, :, None]


def pad_z(box):
    return jnp.pad(box, ((0, 0), (0, 0), (1, 1)))


def trim(box):
    return box[1:-1, 1:-1, :]


def neighbours(padded):
    return [
        padded[2:, 1:-1, 1:-1],
        padded[:-2, 1:-1, 1:-1],
        padded[1:-1, 2:, 1:-1],
        padded[1:-1, :-2, 1:-1],
        padded[1:-1, 1:-1, 2:],
        padded[1:-1, 1:-1, :-2],
    ]


def face_weights(padded_coef, scale):
    centre = padded_coef[1:-1, 1:-1, 1:-1]
    weights = [0.5 * scale * (centre + other) for other in neighbours(padded_coef)]
    diagonal = damping_alpha + weights[0]
    for other in weights[1:]:
        diagonal = diagonal + other
    return (weights, diagonal)


def apply_operator(padded, field, weights, diagonal):
    result = diagonal * field
    for weight, other in zip(weights, neighbours(padded)):
        result = result - weight * other
    return result


def smooth_level(start, right_side, coefficient, scale, extend):
    weights, diagonal = face_weights(extend(coefficient), scale)
    if start is None:
        start = jnp.zeros_like(right_side)
        residual = right_side
    else:
        residual = right_side - apply_operator(extend(start), start, weights, diagonal)
    first_step = residual / (cheb_theta * diagonal)
    first = start + first_step
    residual = right_side - apply_operator(extend(first), first, weights, diagonal)
    second_step = cheb_carry * first_step + cheb_resid * residual / diagonal
    second = first + second_step
    residual = right_side - apply_operator(extend(second), second, weights, diagonal)
    return (second, residual)


def pair_matrix(count):
    rows = jnp.arange(count // 2)[:, None]
    cols = jnp.arange(count)[None, :] // 2
    return (rows == cols).astype(jnp.float32)


def restrict_field(field):
    sx, sy, sz = field.shape
    halves = field.reshape(sx // 2, 2, sy, sz)
    summed = halves[:, 0] + halves[:, 1]
    summed = jnp.einsum(
        "xyZ,zZ->xyz", summed, pair_matrix(sz), precision=lax.Precision.HIGHEST
    )
    pairs_y = jnp.broadcast_to(pair_matrix(sy), (sx // 2, sy // 2, sy))
    summed = jnp.einsum(
        "xyY,xYz->xyz", pairs_y, summed, precision=lax.Precision.HIGHEST
    )
    return summed * 0.125


def coarse_solve(right_side, coefficient, scale, extend):
    weights, diagonal = face_weights(extend(coefficient), scale)
    field = jnp.zeros_like(right_side)
    for repeat in range(COARSE_ITERS):
        field = (
            field
            + jacobi_weight
            * (right_side - apply_operator(extend(field), field, weights, diagonal))
            / diagonal
        )
    leftover = right_side - apply_operator(extend(field), field, weights, diagonal)
    ones_field = jnp.ones_like(right_side)
    image_ones = apply_operator(extend(ones_field), ones_field, weights, diagonal)
    return field + jnp.sum(leftover) / jnp.sum(image_ones)


def extend_all(field):
    return jnp.pad(field, 1)


def smooth_box(start, right_side, coefficient, scale, shape):
    weights, diagonal = face_weights(pad_z(coefficient), scale)
    if start is None:
        start = jnp.zeros_like(right_side)
        residual = right_side
    else:
        residual = right_side - apply_operator(pad_z(start), trim(start), weights, diagonal)
        start = trim(start)
    first_step = residual / (cheb_theta * diagonal)
    inside = inside_mask(shape, 2)
    first = jnp.where(inside, start + first_step, 0.0)
    weights = [trim(w) for w in weights]
    diagonal = trim(diagonal)
    right_side = trim(right_side)
    residual = right_side - apply_operator(pad_z(first), trim(first), weights, diagonal)
    second_step = cheb_carry * trim(first_step) + cheb_resid * residual / diagonal
    second = jnp.where(trim(inside), trim(first) + second_step, 0.0)
    weights = [trim(w) for w in weights]
    diagonal = trim(diagonal)
    residual = trim(right_side) - apply_operator(pad_z(second), trim(second), weights, diagonal)
    return (trim(second), residual)


def collect_grid(right_side, coefficient):
    sx, sy, sz = right_side.shape
    count_x = lax.axis_size("xb")
    count_y = lax.axis_size("yb")
    flat = jnp.concatenate([right_side.reshape(1, -1), coefficient.reshape(1, -1)], axis=1)
    both = lax.all_gather(flat, "yb", axis=0, tiled=True)
    both = lax.all_gather(both, "xb", axis=0, tiled=True)
    size = sx * sy * sz
    return tuple(
        (
            piece.reshape(count_x, count_y, sx, sy, sz)
            .transpose(0, 2, 1, 3, 4)
            .reshape(count_x * sx, count_y * sy, sz)
            for piece in (both[:, :size], both[:, size:])
        )
    )


def own_block(whole, shape):
    start_x = lax.axis_index("xb") * shape[0]
    start_y = lax.axis_index("yb") * shape[1]
    return lax.dynamic_slice(whole, (start_x, start_y, jnp.int32(0)), shape)


def per_device(initial_guess, right_side, coefficient):
    mid_coef = restrict_field(coefficient)
    low_coef = restrict_field(mid_coef)
    low_size = low_coef.shape[0]
    low_first = min(3, low_size)
    assert low_first == 3 or 2 * low_first >= 3
    (guess_b, rhs_b, coef_b, mid_coef_b, low_coef_b), _ = exchange_xy(
        [(initial_guess, 3), (right_side, 2), (coefficient, 3), (mid_coef, 3), (low_coef, low_first, 3)]
    )
    fine, fine_res = smooth_box(guess_b, rhs_b, coef_b, 1.0, right_side.shape)
    mid_rhs = restrict_field(fine_res)
    (mid_rhs_b,), _ = exchange_xy([(mid_rhs, 2)])
    middle, mid_res = smooth_box(None, mid_rhs_b, mid_coef_b, 0.25, mid_rhs.shape)
    low_rhs = restrict_field(mid_res)
    forwards = ()
    if low_first < 3:
        forwards = (
            (low_coef_b, (2 * low_size - 3, low_size), (2 * low_size, low_size + 3)),
        )
    (low_rhs_b,), boxes = exchange_xy([(low_rhs, 2)], forwards)
    if low_first < 3:
        (low_coef_b,) = boxes
    lower, low_res = smooth_box(None, low_rhs_b, low_coef_b, 0.0625, low_rhs.shape)
    coarse_rhs, coarse_coef = collect_grid(restrict_field(low_res), restrict_field(low_coef))
    coarse_whole = coarse_solve(coarse_rhs, coarse_coef, 0.015625, extend_all)
    sx, sy, sz = right_side.shape
    coarse = own_block(coarse_whole, (sx // 8, sy // 8, sz // 8))
    return (fine, middle, lower, coarse)


def solution(mesh):
    placed = (P("xb", "yb", None), P("xb", "yb", None), P("xb", "yb", None))
    return jax.shard_map(
        per_device,
        mesh=mesh,
        in_specs=placed,
        out_specs=(
            P("xb", "yb", None),
            P("xb", "yb", None),
            P("xb", "yb", None),
            P("xb", "yb", None),
        ),
        check_vma=False,
    )
```

```python
import jax
import jax.numpy as jnp
from jax import lax
from jax.sharding import PartitionSpec as P

COARSE_ITERS = 8


damping_alpha = 0.05
cheb_theta = 1.15
cheb_delta = 0.85
cheb_sigma = cheb_theta / cheb_delta
cheb_first = 1.0 / cheb_sigma
cheb_second = 1.0 / (2.0 * cheb_sigma - cheb_first)
cheb_carry = cheb_second * cheb_first
cheb_resid = 2.0 * cheb_second / cheb_delta
jacobi_weight = 0.8


def exchange(items, axis, dim):
    count = lax.axis_size(axis)
    low = [[] for _ in items]
    high = [[] for _ in items]
    reach = max(-(-width // block.shape[dim]) for block, width in items)
    for hop in range(1, reach + 1):
        for sign in (1, -1):
            pieces = []
            owners = []
            for index, (block, width) in enumerate(items):
                size = block.shape[dim]
                rows = min(size, width - (hop - 1) * size)
                if rows <= 0:
                    continue
                begin = size - rows if sign == 1 else 0
                pieces.append(lax.slice_in_dim(block, begin, begin + rows, axis=dim))
                owners.append(index)
            joined = jnp.concatenate(pieces, axis=0)
            if sign == 1:
                pairs = [(i, i + hop) for i in range(count - hop)]
            else:
                pairs = [(i + hop, i) for i in range(count - hop)]
            got = lax.ppermute(joined, axis, pairs)
            offset = 0
            for index, piece in zip(owners, pieces):
                part = lax.slice_in_dim(got, offset, offset + piece.shape[0], axis=0)
                offset += piece.shape[0]
                if sign == 1:
                    low[index].insert(0, part)
                else:
                    high[index].append(part)
    return [
        jnp.concatenate(low[i] + [block] + high[i], axis=dim)
        for i, (block, width) in enumerate(items)
    ]


def exchange_xy(items):
    extended = exchange([(block, 3) for block, _ in items], "yb", 1)
    return exchange([(block, item[1]) for block, item in zip(extended, items)], "xb", 0)


def inside_mask(shape, halo):
    sx, sy, _ = shape
    gx = lax.axis_index("xb") * sx - halo + jnp.arange(sx + 2 * halo)
    gy = lax.axis_index("yb") * sy - halo + jnp.arange(sy + 2 * halo)
    in_x = (gx >= 0) & (gx < sx * lax.axis_size("xb"))
    in_y = (gy >= 0) & (gy < sy * lax.axis_size("yb"))
    return in_x[:, None, None] & in_y[None, :, None]


def pad_z(box):
    return jnp.pad(box, ((0, 0), (0, 0), (1, 1)))


def trim(box):
    return box[1:-1, 1:-1, :]


def neighbours(padded):
    return [
        padded[2:, 1:-1, 1:-1],
        padded[:-2, 1:-1, 1:-1],
        padded[1:-1, 2:, 1:-1],
        padded[1:-1, :-2, 1:-1],
        padded[1:-1, 1:-1, 2:],
        padded[1:-1, 1:-1, :-2],
    ]


def face_weights(padded_coef, scale):
    centre = padded_coef[1:-1, 1:-1, 1:-1]
    weights = [0.5 * scale * (centre + other) for other in neighbours(padded_coef)]
    diagonal = damping_alpha + weights[0]
    for other in weights[1:]:
        diagonal = diagonal + other
    return (weights, diagonal)


def apply_operator(padded, field, weights, diagonal):
    result = diagonal * field
    for weight, other in zip(weights, neighbours(padded)):
        result = result - weight * other
    return result


def smooth_level(start, right_side, coefficient, scale, extend):
    weights, diagonal = face_weights(extend(coefficient), scale)
    if start is None:
        start = jnp.zeros_like(right_side)
        residual = right_side
    else:
        residual = right_side - apply_operator(extend(start), start, weights, diagonal)
    first_step = residual / (cheb_theta * diagonal)
    first = start + first_step
    residual = right_side - apply_operator(extend(first), first, weights, diagonal)
    second_step = cheb_carry * first_step + cheb_resid * residual / diagonal
    second = first + second_step
    residual = right_side - apply_operator(extend(second), second, weights, diagonal)
    return (second, residual)


def pair_matrix(count):
    rows = jnp.arange(count // 2)[:, None]
    cols = jnp.arange(count)[None, :] // 2
    return (rows == cols).astype(jnp.float32)


def restrict_field(field):
    sx, sy, sz = field.shape
    halves = field.reshape(sx // 2, 2, sy, sz)
    summed = halves[:, 0] + halves[:, 1]
    summed = jnp.einsum(
        "xyZ,zZ->xyz", summed, pair_matrix(sz), precision=lax.Precision.HIGHEST
    )
    pairs_y = jnp.broadcast_to(pair_matrix(sy), (sx // 2, sy // 2, sy))
    summed = jnp.einsum(
        "xyY,xYz->xyz", pairs_y, summed, precision=lax.Precision.HIGHEST
    )
    return summed * 0.125


def coarse_solve(right_side, coefficient, scale, extend):
    weights, diagonal = face_weights(extend(coefficient), scale)
    field = jnp.zeros_like(right_side)
    for repeat in range(COARSE_ITERS):
        field = (
            field
            + jacobi_weight
            * (right_side - apply_operator(extend(field), field, weights, diagonal))
            / diagonal
        )
    leftover = right_side - apply_operator(extend(field), field, weights, diagonal)
    ones_field = jnp.ones_like(right_side)
    image_ones = apply_operator(extend(ones_field), ones_field, weights, diagonal)
    return field + jnp.sum(leftover) / jnp.sum(image_ones)


def extend_all(field):
    return jnp.pad(field, 1)


def smooth_box(start, right_side, coefficient, scale, shape):
    weights, diagonal = face_weights(pad_z(coefficient), scale)
    if start is None:
        start = jnp.zeros_like(right_side)
        residual = right_side
    else:
        residual = right_side - apply_operator(pad_z(start), trim(start), weights, diagonal)
        start = trim(start)
    first_step = residual / (cheb_theta * diagonal)
    first = jnp.where(inside_mask(shape, 2), start + first_step, 0.0)
    weights = [trim(w) for w in weights]
    diagonal = trim(diagonal)
    right_side = trim(right_side)
    residual = right_side - apply_operator(pad_z(first), trim(first), weights, diagonal)
    second_step = cheb_carry * trim(first_step) + cheb_resid * residual / diagonal
    second = jnp.where(inside_mask(shape, 1), trim(first) + second_step, 0.0)
    weights = [trim(w) for w in weights]
    diagonal = trim(diagonal)
    residual = trim(right_side) - apply_operator(pad_z(second), trim(second), weights, diagonal)
    return (trim(second), residual)


def collect_grid(right_side, coefficient):
    sx, sy, sz = right_side.shape
    count_x = lax.axis_size("xb")
    count_y = lax.axis_size("yb")
    flat = jnp.concatenate([right_side.reshape(1, -1), coefficient.reshape(1, -1)], axis=1)
    both = lax.all_gather(flat, ("xb", "yb"), axis=0, tiled=True)
    size = sx * sy * sz
    return tuple(
        (
            piece.reshape(count_x, count_y, sx, sy, sz)
            .transpose(0, 2, 1, 3, 4)
            .reshape(count_x * sx, count_y * sy, sz)
            for piece in (both[:, :size], both[:, size:])
        )
    )


def own_block(whole, shape):
    start_x = lax.axis_index("xb") * shape[0]
    start_y = lax.axis_index("yb") * shape[1]
    return lax.dynamic_slice(whole, (start_x, start_y, jnp.int32(0)), shape)


def per_device(initial_guess, right_side, coefficient):
    guess_b, rhs_b, coef_b = exchange_xy([(initial_guess, 3), (right_side, 2), (coefficient, 3)])
    fine, fine_res = smooth_box(guess_b, rhs_b[:, 1:-1], coef_b, 1.0, right_side.shape)
    mid_coef = restrict_field(coefficient)
    mid_rhs = restrict_field(fine_res)
    mid_rhs_b, mid_coef_b = exchange_xy([(mid_rhs, 2), (mid_coef, 3)])
    middle, mid_res = smooth_box(None, mid_rhs_b[:, 1:-1], mid_coef_b, 0.25, mid_rhs.shape)
    low_coef = restrict_field(mid_coef)
    low_rhs = restrict_field(mid_res)
    low_rhs_b, low_coef_b = exchange_xy([(low_rhs, 2), (low_coef, 3)])
    lower, low_res = smooth_box(None, low_rhs_b[:, 1:-1], low_coef_b, 0.0625, low_rhs.shape)
    coarse_rhs, coarse_coef = collect_grid(restrict_field(low_res), restrict_field(low_coef))
    coarse_whole = coarse_solve(coarse_rhs, coarse_coef, 0.015625, extend_all)
    sx, sy, sz = right_side.shape
    coarse = own_block(coarse_whole, (sx // 8, sy // 8, sz // 8))
    return (fine, middle, lower, coarse)


def solution(mesh):
    placed = (P("xb", "yb", None), P("xb", "yb", None), P("xb", "yb", None))
    return jax.shard_map(
        per_device,
        mesh=mesh,
        in_specs=placed,
        out_specs=(
            P("xb", "yb", None),
            P("xb", "yb", None),
            P("xb", "yb", None),
            P("xb", "yb", None),
        ),
        check_vma=False,
    )
```

```python
import jax
import jax.numpy as jnp
from jax import lax
from jax.sharding import PartitionSpec as P

COARSE_ITERS = 8


damping_alpha = 0.05
cheb_theta = 1.15
cheb_delta = 0.85
cheb_sigma = cheb_theta / cheb_delta
cheb_first = 1.0 / cheb_sigma
cheb_second = 1.0 / (2.0 * cheb_sigma - cheb_first)
cheb_carry = cheb_second * cheb_first
cheb_resid = 2.0 * cheb_second / cheb_delta
jacobi_weight = 0.8


def exchange(items, axis, dim, forwards=()):
    count = lax.axis_size(axis)
    low = [[] for _ in items]
    high = [[] for _ in items]
    boxes = [box for box, _, _ in forwards]
    reach = max(-(-width // block.shape[dim]) for block, width in items)
    for hop in range(1, reach + 1):
        for sign in (1, -1):
            pieces = []
            owners = []
            for index, (block, width) in enumerate(items):
                size = block.shape[dim]
                rows = min(size, width - (hop - 1) * size)
                if rows <= 0:
                    continue
                begin = size - rows if sign == 1 else 0
                pieces.append(lax.slice_in_dim(block, begin, begin + rows, axis=dim))
                owners.append(index)
            if hop == 1:
                for index, (box, rows_low, rows_high) in enumerate(forwards):
                    rows = rows_low if sign == 1 else rows_high
                    pieces.append(lax.slice_in_dim(box, rows[0], rows[1], axis=dim))
                    owners.append(-1 - index)
            common = [max(p.shape[d] for p in pieces) for d in (1, 2)]
            joined = jnp.concatenate(
                [
                    jnp.pad(p, ((0, 0), (0, common[0] - p.shape[1]), (0, common[1] - p.shape[2])))
                    for p in pieces
                ],
                axis=0,
            )
            if sign == 1:
                pairs = [(i, i + hop) for i in range(count - hop)]
            else:
                pairs = [(i + hop, i) for i in range(count - hop)]
            got = lax.ppermute(joined, axis, pairs)
            offset = 0
            for index, piece in zip(owners, pieces):
                part = got[offset : offset + piece.shape[0], : piece.shape[1], : piece.shape[2]]
                offset += piece.shape[0]
                if index < 0:
                    box = boxes[-1 - index]
                    parts = [part, box] if sign == 1 else [box, part]
                    boxes[-1 - index] = jnp.concatenate(parts, axis=dim)
                elif sign == 1:
                    low[index].insert(0, part)
                else:
                    high[index].append(part)
    extended = [
        jnp.concatenate(low[i] + [block] + high[i], axis=dim)
        for i, (block, width) in enumerate(items)
    ]
    return extended, boxes


def pad_z(box):
    return jnp.pad(box, ((0, 0), (0, 0), (1, 1)))


def trim(box):
    return box[1:-1, 1:-1, :]


def neighbours(padded):
    return [
        padded[2:, 1:-1, 1:-1],
        padded[:-2, 1:-1, 1:-1],
        padded[1:-1, 2:, 1:-1],
        padded[1:-1, :-2, 1:-1],
        padded[1:-1, 1:-1, 2:],
        padded[1:-1, 1:-1, :-2],
    ]


def face_weights(padded_coef, scale):
    centre = padded_coef[1:-1, 1:-1, 1:-1]
    weights = [0.5 * scale * (centre + other) for other in neighbours(padded_coef)]
    diagonal = damping_alpha + weights[0]
    for other in weights[1:]:
        diagonal = diagonal + other
    return (weights, diagonal)


def apply_operator(padded, field, weights, diagonal):
    result = diagonal * field
    for weight, other in zip(weights, neighbours(padded)):
        result = result - weight * other
    return result


def smooth_level(start, right_side, coefficient, scale, extend):
    weights, diagonal = face_weights(extend(coefficient), scale)
    if start is None:
        start = jnp.zeros_like(right_side)
        residual = right_side
    else:
        residual = right_side - apply_operator(extend(start), start, weights, diagonal)
    first_step = residual / (cheb_theta * diagonal)
    first = start + first_step
    residual = right_side - apply_operator(extend(first), first, weights, diagonal)
    second_step = cheb_carry * first_step + cheb_resid * residual / diagonal
    second = first + second_step
    residual = right_side - apply_operator(extend(second), second, weights, diagonal)
    return (second, residual)


def pair_matrix(count):
    rows = jnp.arange(count // 2)[:, None]
    cols = jnp.arange(count)[None, :] // 2
    return (rows == cols).astype(jnp.float32)


def restrict_field(field):
    sx, sy, sz = field.shape
    halves = field.reshape(sx // 2, 2, sy, sz)
    summed = halves[:, 0] + halves[:, 1]
    summed = jnp.einsum(
        "xyZ,zZ->xyz", summed, pair_matrix(sz), precision=lax.Precision.HIGHEST
    )
    pairs_y = jnp.broadcast_to(pair_matrix(sy), (sx // 2, sy // 2, sy))
    summed = jnp.einsum(
        "xyY,xYz->xyz", pairs_y, summed, precision=lax.Precision.HIGHEST
    )
    return summed * 0.125


def coarse_solve(right_side, coefficient, scale, extend):
    weights, diagonal = face_weights(extend(coefficient), scale)
    field = jnp.zeros_like(right_side)
    for repeat in range(COARSE_ITERS):
        field = (
            field
            + jacobi_weight
            * (right_side - apply_operator(extend(field), field, weights, diagonal))
            / diagonal
        )
    leftover = right_side - apply_operator(extend(field), field, weights, diagonal)
    ones_field = jnp.ones_like(right_side)
    image_ones = apply_operator(extend(ones_field), ones_field, weights, diagonal)
    return field + jnp.sum(leftover) / jnp.sum(image_ones)


def extend_all(field):
    return jnp.pad(field, 1)


def box_weights(padded_coef, scale):
    centre = padded_coef[1:-1, 1:-1, 1:-1]
    outside = centre == 0.0
    weights = [
        jnp.where(outside, 0.0, 0.5 * scale * (centre + other))
        for other in neighbours(padded_coef)
    ]
    diagonal = damping_alpha + weights[0]
    for other in weights[1:]:
        diagonal = diagonal + other
    return (weights, diagonal)


def smooth_box(start, right_side, coefficient, scale):
    weights, diagonal = box_weights(pad_z(coefficient), scale)
    if start is None:
        start = jnp.zeros_like(right_side)
        residual = right_side
    else:
        residual = right_side - apply_operator(pad_z(start), trim(start), weights, diagonal)
        start = trim(start)
    first_step = residual / (cheb_theta * diagonal)
    first = start + first_step
    weights = [trim(w) for w in weights]
    diagonal = trim(diagonal)
    right_side = trim(right_side)
    residual = right_side - apply_operator(pad_z(first), trim(first), weights, diagonal)
    second_step = cheb_carry * trim(first_step) + cheb_resid * residual / diagonal
    second = trim(first) + second_step
    weights = [trim(w) for w in weights]
    diagonal = trim(diagonal)
    residual = trim(right_side) - apply_operator(pad_z(second), trim(second), weights, diagonal)
    return (trim(second), residual)


def collect_grid(right_side, coefficient):
    sx, sy, sz = right_side.shape
    count_x = lax.axis_size("xb")
    count_y = lax.axis_size("yb")
    flat = jnp.concatenate([right_side.reshape(1, -1), coefficient.reshape(1, -1)], axis=1)
    both = lax.all_gather(flat, ("xb", "yb"), axis=0, tiled=True)
    size = sx * sy * sz
    return tuple(
        (
            piece.reshape(count_x, count_y, sx, sy, sz)
            .transpose(0, 2, 1, 3, 4)
            .reshape(count_x * sx, count_y * sy, sz)
            for piece in (both[:, :size], both[:, size:])
        )
    )


def own_block(whole, shape):
    start_x = lax.axis_index("xb") * shape[0]
    start_y = lax.axis_index("yb") * shape[1]
    return lax.dynamic_slice(whole, (start_x, start_y, jnp.int32(0)), shape)


def per_device(initial_guess, right_side, coefficient):
    mid_coef = restrict_field(coefficient)
    low_coef = restrict_field(mid_coef)
    low_size = low_coef.shape[0]
    low_first = min(3, low_size)
    assert low_first == 3 or 2 * low_size >= 3
    guess_b, rhs_b, coef_b, low_coef_b = exchange(
        [(initial_guess, 3), (right_side, 3), (coefficient, 3), (low_coef, 3)], "yb", 1
    )[0]
    guess_b, rhs_b, coef_b = exchange([(guess_b, 3), (rhs_b, 2), (coef_b, 3)], "xb", 0)[0]
    fine, fine_res = smooth_box(guess_b, rhs_b[:, 1:-1], coef_b, 1.0)
    mid_rhs = restrict_field(fine_res)
    mid_rhs_b, mid_coef_b = exchange([(mid_rhs, 3), (mid_coef, 3)], "yb", 1)[0]
    mid_rhs_b, mid_coef_b, low_coef_b = exchange(
        [(mid_rhs_b, 2), (mid_coef_b, 3), (low_coef_b, low_first)], "xb", 0
    )[0]
    middle, mid_res = smooth_box(None, mid_rhs_b[:, 1:-1], mid_coef_b, 0.25)
    low_rhs = restrict_field(mid_res)
    (low_rhs_b,) = exchange([(low_rhs, 3)], "yb", 1)[0]
    forwards = ()
    if low_first < 3:
        forwards = ((low_coef_b, (2 * low_size - 3, low_size), (2 * low_size, low_size + 3)),)
    (low_rhs_b,), boxes = exchange([(low_rhs_b, 2)], "xb", 0, forwards)
    if low_first < 3:
        (low_coef_b,) = boxes
    lower, low_res = smooth_box(None, low_rhs_b[:, 1:-1], low_coef_b, 0.0625)
    coarse_rhs, coarse_coef = collect_grid(restrict_field(low_res), restrict_field(low_coef))
    coarse_whole = coarse_solve(coarse_rhs, coarse_coef, 0.015625, extend_all)
    sx, sy, sz = right_side.shape
    coarse = own_block(coarse_whole, (sx // 8, sy // 8, sz // 8))
    return (fine, middle, lower, coarse)


def solution(mesh):
    placed = (P("xb", "yb", None), P("xb", "yb", None), P("xb", "yb", None))
    return jax.shard_map(
        per_device,
        mesh=mesh,
        in_specs=placed,
        out_specs=(
            P("xb", "yb", None),
            P("xb", "yb", None),
            P("xb", "yb", None),
            P("xb", "yb", None),
        ),
        check_vma=False,
    )
```

```python
import jax
import jax.numpy as jnp
from jax import lax
from jax.sharding import PartitionSpec as P

COARSE_ITERS = 8


damping_alpha = 0.05
cheb_theta = 1.15
cheb_delta = 0.85
cheb_sigma = cheb_theta / cheb_delta
cheb_first = 1.0 / cheb_sigma
cheb_second = 1.0 / (2.0 * cheb_sigma - cheb_first)
cheb_carry = cheb_second * cheb_first
cheb_resid = 2.0 * cheb_second / cheb_delta
jacobi_weight = 0.8


def exchange(items, axis, dim, forwards=()):
    count = lax.axis_size(axis)
    low = [[] for _ in items]
    high = [[] for _ in items]
    boxes = [box for box, _, _ in forwards]
    reach = max(-(-width // block.shape[dim]) for block, width in items)
    for hop in range(1, reach + 1):
        for sign in (1, -1):
            pieces = []
            owners = []
            for index, (block, width) in enumerate(items):
                size = block.shape[dim]
                rows = min(size, width - (hop - 1) * size)
                if rows <= 0:
                    continue
                begin = size - rows if sign == 1 else 0
                pieces.append(lax.slice_in_dim(block, begin, begin + rows, axis=dim))
                owners.append(index)
            if hop == 1:
                for index, (box, rows_low, rows_high) in enumerate(forwards):
                    rows = rows_low if sign == 1 else rows_high
                    pieces.append(lax.slice_in_dim(box, rows[0], rows[1], axis=dim))
                    owners.append(-1 - index)
            common = [max(p.shape[d] for p in pieces) for d in (1, 2)]
            joined = jnp.concatenate(
                [
                    jnp.pad(p, ((0, 0), (0, common[0] - p.shape[1]), (0, common[1] - p.shape[2])))
                    for p in pieces
                ],
                axis=0,
            )
            if sign == 1:
                pairs = [(i, i + hop) for i in range(count - hop)]
            else:
                pairs = [(i + hop, i) for i in range(count - hop)]
            got = lax.ppermute(joined, axis, pairs)
            offset = 0
            for index, piece in zip(owners, pieces):
                part = got[offset : offset + piece.shape[0], : piece.shape[1], : piece.shape[2]]
                offset += piece.shape[0]
                if index < 0:
                    box = boxes[-1 - index]
                    parts = [part, box] if sign == 1 else [box, part]
                    boxes[-1 - index] = jnp.concatenate(parts, axis=dim)
                elif sign == 1:
                    low[index].insert(0, part)
                else:
                    high[index].append(part)
    extended = [
        jnp.concatenate(low[i] + [block] + high[i], axis=dim)
        for i, (block, width) in enumerate(items)
    ]
    return extended, boxes


def pad_z(box):
    return jnp.pad(box, ((0, 0), (0, 0), (1, 1)))


def trim(box):
    return box[1:-1, 1:-1, :]


def neighbours(padded):
    return [
        padded[2:, 1:-1, 1:-1],
        padded[:-2, 1:-1, 1:-1],
        padded[1:-1, 2:, 1:-1],
        padded[1:-1, :-2, 1:-1],
        padded[1:-1, 1:-1, 2:],
        padded[1:-1, 1:-1, :-2],
    ]


def face_weights(padded_coef, scale):
    centre = padded_coef[1:-1, 1:-1, 1:-1]
    weights = [0.5 * scale * (centre + other) for other in neighbours(padded_coef)]
    diagonal = damping_alpha + weights[0]
    for other in weights[1:]:
        diagonal = diagonal + other
    return (weights, diagonal)


def apply_operator(padded, field, weights, diagonal):
    result = diagonal * field
    for weight, other in zip(weights, neighbours(padded)):
        result = result - weight * other
    return result


def smooth_level(start, right_side, coefficient, scale, extend):
    weights, diagonal = face_weights(extend(coefficient), scale)
    if start is None:
        start = jnp.zeros_like(right_side)
        residual = right_side
    else:
        residual = right_side - apply_operator(extend(start), start, weights, diagonal)
    first_step = residual / (cheb_theta * diagonal)
    first = start + first_step
    residual = right_side - apply_operator(extend(first), first, weights, diagonal)
    second_step = cheb_carry * first_step + cheb_resid * residual / diagonal
    second = first + second_step
    residual = right_side - apply_operator(extend(second), second, weights, diagonal)
    return (second, residual)


def pair_matrix(count):
    rows = jnp.arange(count // 2)[:, None]
    cols = jnp.arange(count)[None, :] // 2
    return (rows == cols).astype(jnp.float32)


def restrict_field(field):
    sx, sy, sz = field.shape
    halves = field.reshape(sx // 2, 2, sy, sz)
    summed = halves[:, 0] + halves[:, 1]
    summed = jnp.einsum(
        "xyZ,zZ->xyz", summed, pair_matrix(sz), precision=lax.Precision.HIGHEST
    )
    pairs_y = jnp.broadcast_to(pair_matrix(sy), (sx // 2, sy // 2, sy))
    summed = jnp.einsum(
        "xyY,xYz->xyz", pairs_y, summed, precision=lax.Precision.HIGHEST
    )
    return summed * 0.125


def coarse_solve(right_side, coefficient, scale, extend):
    weights, diagonal = face_weights(extend(coefficient), scale)
    field = jnp.zeros_like(right_side)
    for repeat in range(COARSE_ITERS):
        field = (
            field
            + jacobi_weight
            * (right_side - apply_operator(extend(field), field, weights, diagonal))
            / diagonal
        )
    leftover = right_side - apply_operator(extend(field), field, weights, diagonal)
    ones_field = jnp.ones_like(right_side)
    image_ones = apply_operator(extend(ones_field), ones_field, weights, diagonal)
    return field + jnp.sum(leftover) / jnp.sum(image_ones)


def extend_all(field):
    return jnp.pad(field, 1)


def box_weights(padded_coef, scale):
    centre = padded_coef[1:-1, 1:-1, 1:-1]
    outside = centre == 0.0
    weights = [
        jnp.where(outside, 0.0, 0.5 * scale * (centre + other))
        for other in neighbours(padded_coef)
    ]
    diagonal = damping_alpha + weights[0]
    for other in weights[1:]:
        diagonal = diagonal + other
    return (weights, diagonal)


def smooth_box(start, right_side, coefficient, scale):
    weights, diagonal = box_weights(pad_z(coefficient), scale)
    if start is None:
        start = jnp.zeros_like(right_side)
        residual = right_side
    else:
        residual = right_side - apply_operator(pad_z(start), trim(start), weights, diagonal)
        start = trim(start)
    first_step = residual / (cheb_theta * diagonal)
    first = start + first_step
    weights = [trim(w) for w in weights]
    diagonal = trim(diagonal)
    right_side = trim(right_side)
    residual = right_side - apply_operator(pad_z(first), trim(first), weights, diagonal)
    second_step = cheb_carry * trim(first_step) + cheb_resid * residual / diagonal
    second = trim(first) + second_step
    weights = [trim(w) for w in weights]
    diagonal = trim(diagonal)
    residual = trim(right_side) - apply_operator(pad_z(second), trim(second), weights, diagonal)
    return (trim(second), residual)


def collect_grid(right_side, coefficient):
    sx, sy, sz = right_side.shape
    count_x = lax.axis_size("xb")
    count_y = lax.axis_size("yb")
    flat = jnp.concatenate([right_side.reshape(1, -1), coefficient.reshape(1, -1)], axis=1)
    both = lax.all_gather(flat, ("xb", "yb"), axis=0, tiled=True)
    size = sx * sy * sz
    return tuple(
        (
            piece.reshape(count_x, count_y, sx, sy, sz)
            .transpose(0, 2, 1, 3, 4)
            .reshape(count_x * sx, count_y * sy, sz)
            for piece in (both[:, :size], both[:, size:])
        )
    )


def own_block(whole, shape):
    start_x = lax.axis_index("xb") * shape[0]
    start_y = lax.axis_index("yb") * shape[1]
    return lax.dynamic_slice(whole, (start_x, start_y, jnp.int32(0)), shape)


def per_device(initial_guess, right_side, coefficient):
    mid_coef = restrict_field(coefficient)
    low_coef = restrict_field(mid_coef)
    low_size = low_coef.shape[0]
    low_first = min(3, low_size)
    assert low_first == 3 or 2 * low_size >= 3
    guess_b, rhs_b, coef_b, mid_coef_b, low_coef_b = exchange(
        [(initial_guess, 7), (right_side, 7), (coefficient, 7), (mid_coef, 3), (low_coef, 3)],
        "yb",
        1,
    )[0]
    guess_b, rhs_b, coef_b = exchange([(guess_b, 3), (rhs_b, 2), (coef_b, 3)], "xb", 0)[0]
    fine, fine_res = smooth_box(guess_b, rhs_b[:, 1:-1], coef_b, 1.0)
    fine = fine[:, 4:-4]
    mid_rhs = restrict_field(fine_res)
    mid_rhs_b, mid_coef_b, low_coef_b = exchange(
        [(mid_rhs, 2), (mid_coef_b, 3), (low_coef_b, low_first)], "xb", 0
    )[0]
    middle, mid_res = smooth_box(None, mid_rhs_b, mid_coef_b, 0.25)
    low_rhs = restrict_field(mid_res)
    (low_rhs_b,) = exchange([(low_rhs, 3)], "yb", 1)[0]
    forwards = ()
    if low_first < 3:
        forwards = ((low_coef_b, (2 * low_size - 3, low_size), (2 * low_size, low_size + 3)),)
    (low_rhs_b,), boxes = exchange([(low_rhs_b, 2)], "xb", 0, forwards)
    if low_first < 3:
        (low_coef_b,) = boxes
    lower, low_res = smooth_box(None, low_rhs_b[:, 1:-1], low_coef_b, 0.0625)
    coarse_rhs, coarse_coef = collect_grid(restrict_field(low_res), restrict_field(low_coef))
    coarse_whole = coarse_solve(coarse_rhs, coarse_coef, 0.015625, extend_all)
    sx, sy, sz = right_side.shape
    coarse = own_block(coarse_whole, (sx // 8, sy // 8, sz // 8))
    return (fine, middle, lower, coarse)


def solution(mesh):
    placed = (P("xb", "yb", None), P("xb", "yb", None), P("xb", "yb", None))
    return jax.shard_map(
        per_device,
        mesh=mesh,
        in_specs=placed,
        out_specs=(
            P("xb", "yb", None),
            P("xb", "yb", None),
            P("xb", "yb", None),
            P("xb", "yb", None),
        ),
        check_vma=False,
    )
```

```python
import jax
import jax.numpy as jnp
from jax import lax
from jax.sharding import PartitionSpec as P


COARSE_ITERS = 8


damping_alpha = 0.05
cheb_theta = 1.15
cheb_delta = 0.85
cheb_sigma = cheb_theta / cheb_delta
cheb_first = 1.0 / cheb_sigma
cheb_second = 1.0 / (2.0 * cheb_sigma - cheb_first)
cheb_carry = cheb_second * cheb_first
cheb_resid = 2.0 * cheb_second / cheb_delta
jacobi_weight = 0.8


def exchange(items, axis, dim, forwards=()):
    count = lax.axis_size(axis)
    low = [[] for _ in items]
    high = [[] for _ in items]
    boxes = [box for box, _, _ in forwards]
    reach = max(-(-width // block.shape[dim]) for block, width in items)
    for hop in range(1, reach + 1):
        for sign in (1, -1):
            pieces = []
            owners = []
            for index, (block, width) in enumerate(items):
                size = block.shape[dim]
                rows = min(size, width - (hop - 1) * size)
                if rows <= 0:
                    continue
                begin = size - rows if sign == 1 else 0
                pieces.append(lax.slice_in_dim(block, begin, begin + rows, axis=dim))
                owners.append(index)
            if hop == 1:
                for index, (box, rows_low, rows_high) in enumerate(forwards):
                    rows = rows_low if sign == 1 else rows_high
                    pieces.append(lax.slice_in_dim(box, rows[0], rows[1], axis=dim))
                    owners.append(-1 - index)
            common = [max(p.shape[d] for p in pieces) for d in (1, 2)]
            joined = jnp.concatenate(
                [
                    jnp.pad(p, ((0, 0), (0, common[0] - p.shape[1]), (0, common[1] - p.shape[2])))
                    for p in pieces
                ],
                axis=0,
            )
            if sign == 1:
                pairs = [(i, i + hop) for i in range(count - hop)]
            else:
                pairs = [(i + hop, i) for i in range(count - hop)]
            got = lax.ppermute(joined, axis, pairs)
            offset = 0
            for index, piece in zip(owners, pieces):
                part = got[offset : offset + piece.shape[0], : piece.shape[1], : piece.shape[2]]
                offset += piece.shape[0]
                if index < 0:
                    box = boxes[-1 - index]
                    parts = [part, box] if sign == 1 else [box, part]
                    boxes[-1 - index] = jnp.concatenate(parts, axis=dim)
                elif sign == 1:
                    low[index].insert(0, part)
                else:
                    high[index].append(part)
    extended = [
        jnp.concatenate(low[i] + [block] + high[i], axis=dim)
        for i, (block, width) in enumerate(items)
    ]
    return extended, boxes


def send(pieces, axis, pairs):
    common = [max(p.shape[d] for p in pieces) for d in (1, 2)]
    joined = jnp.concatenate(
        [
            jnp.pad(p, ((0, 0), (0, common[0] - p.shape[1]), (0, common[1] - p.shape[2])))
            for p in pieces
        ],
        axis=0,
    )
    got = lax.ppermute(joined, axis, pairs)
    parts = []
    offset = 0
    for piece in pieces:
        parts.append(got[offset : offset + piece.shape[0], : piece.shape[1], : piece.shape[2]])
        offset += piece.shape[0]
    return parts


def exchange_once(items, extras, forwards=()):
    count_x = lax.axis_size("xb")
    count_y = lax.axis_size("yb")
    boxes = []
    faces = {}
    for sign in (1, -1):
        pairs = [(i, i + 1) for i in range(count_x - 1)]
        if sign == -1:
            pairs = [(j, i) for i, j in pairs]
        pieces = []
        for block, wx, wy in items:
            size = block.shape[0]
            begin = size - wx if sign == 1 else 0
            pieces.append(block[begin : begin + wx])
        for box, rows_low, rows_high in forwards:
            rows = rows_low if sign == 1 else rows_high
            pieces.append(box[rows[0] : rows[1]])
        faces[("x", sign)] = send(pieces, "xb", pairs)
    for sign in (1, -1):
        pairs = [(i, i + 1) for i in range(count_y - 1)]
        if sign == -1:
            pairs = [(j, i) for i, j in pairs]
        pieces = []
        for block, _, wy in list(items) + [(b, 0, w) for b, w in extras]:
            size = block.shape[1]
            begin = size - wy if sign == 1 else 0
            pieces.append(block[:, begin : begin + wy])
        faces[("y", sign)] = send(pieces, "yb", pairs)
    for sx in (1, -1):
        for sy in (1, -1):
            pairs = []
            for a in range(count_x):
                for b in range(count_y):
                    if 0 <= a + sx < count_x and 0 <= b + sy < count_y:
                        pairs.append((a * count_y + b, (a + sx) * count_y + (b + sy)))
            pieces = []
            for block, wx, wy in items:
                bx, by = block.shape[0], block.shape[1]
                x0 = bx - wx if sx == 1 else 0
                y0 = by - wy if sy == 1 else 0
                pieces.append(block[x0 : x0 + wx, y0 : y0 + wy])
            faces[(sx, sy)] = send(pieces, ("xb", "yb"), pairs)
    for index, (block, wx, wy) in enumerate(items):
        low = jnp.concatenate(
            [faces[(1, 1)][index], faces[("x", 1)][index], faces[(1, -1)][index]], axis=1
        )
        middle = jnp.concatenate(
            [faces[("y", 1)][index], block, faces[("y", -1)][index]], axis=1
        )
        high = jnp.concatenate(
            [faces[(-1, 1)][index], faces[("x", -1)][index], faces[(-1, -1)][index]], axis=1
        )
        boxes.append(jnp.concatenate([low, middle, high], axis=0))
    for index, (block, wy) in enumerate(extras):
        index += len(items)
        boxes.append(
            jnp.concatenate([faces[("y", 1)][index], block, faces[("y", -1)][index]], axis=1)
        )
    for index, (box, _, _) in enumerate(forwards):
        index += len(items)
        boxes.append(
            jnp.concatenate([faces[("x", 1)][index], box, faces[("x", -1)][index]], axis=0)
        )
    return boxes


def pad_z(box):
    return jnp.pad(box, ((0, 0), (0, 0), (1, 1)))


def trim(box):
    return box[1:-1, 1:-1, :]


def neighbours(padded):
    return [
        padded[2:, 1:-1, 1:-1],
        padded[:-2, 1:-1, 1:-1],
        padded[1:-1, 2:, 1:-1],
        padded[1:-1, :-2, 1:-1],
        padded[1:-1, 1:-1, 2:],
        padded[1:-1, 1:-1, :-2],
    ]


def face_weights(padded_coef, scale):
    centre = padded_coef[1:-1, 1:-1, 1:-1]
    weights = [0.5 * scale * (centre + other) for other in neighbours(padded_coef)]
    diagonal = damping_alpha + weights[0]
    for other in weights[1:]:
        diagonal = diagonal + other
    return (weights, diagonal)


def apply_operator(padded, field, weights, diagonal):
    result = diagonal * field
    for weight, other in zip(weights, neighbours(padded)):
        result = result - weight * other
    return result


def pair_matrix(count):
    rows = jnp.arange(count // 2)[:, None]
    cols = jnp.arange(count)[None, :] // 2
    return (rows == cols).astype(jnp.float32)


def restrict_field(field):
    sx, sy, sz = field.shape
    halves = field.reshape(sx // 2, 2, sy, sz)
    summed = halves[:, 0] + halves[:, 1]
    summed = jnp.einsum(
        "xyZ,zZ->xyz", summed, pair_matrix(sz), precision=lax.Precision.HIGHEST
    )
    pairs_y = jnp.broadcast_to(pair_matrix(sy), (sx // 2, sy // 2, sy))
    summed = jnp.einsum(
        "xyY,xYz->xyz", pairs_y, summed, precision=lax.Precision.HIGHEST
    )
    return summed * 0.125


def coarse_solve(right_side, coefficient, scale, extend):
    weights, diagonal = face_weights(extend(coefficient), scale)
    field = jnp.zeros_like(right_side)
    for _ in range(COARSE_ITERS):
        field = (
            field
            + jacobi_weight
            * (right_side - apply_operator(extend(field), field, weights, diagonal))
            / diagonal
        )
    leftover = right_side - apply_operator(extend(field), field, weights, diagonal)
    ones_field = jnp.ones_like(right_side)
    image_ones = apply_operator(extend(ones_field), ones_field, weights, diagonal)
    return field + jnp.sum(leftover) / jnp.sum(image_ones)


def extend_all(field):
    return jnp.pad(field, 1)


def box_weights(padded_coef, scale):
    centre = padded_coef[1:-1, 1:-1, 1:-1]
    outside = centre == 0.0
    weights = [
        jnp.where(outside, 0.0, 0.5 * scale * (centre + other))
        for other in neighbours(padded_coef)
    ]
    diagonal = damping_alpha + weights[0]
    for other in weights[1:]:
        diagonal = diagonal + other
    return (weights, diagonal)


def smooth_box(start, right_side, coefficient, scale):
    weights, diagonal = box_weights(pad_z(coefficient), scale)
    if start is None:
        start = jnp.zeros_like(right_side)
        residual = right_side
    else:
        residual = right_side - apply_operator(pad_z(start), trim(start), weights, diagonal)
        start = trim(start)
    first_step = residual / (cheb_theta * diagonal)
    first = start + first_step
    weights = [trim(w) for w in weights]
    diagonal = trim(diagonal)
    right_side = trim(right_side)
    residual = right_side - apply_operator(pad_z(first), trim(first), weights, diagonal)
    second_step = cheb_carry * trim(first_step) + cheb_resid * residual / diagonal
    second = trim(first) + second_step
    weights = [trim(w) for w in weights]
    diagonal = trim(diagonal)
    residual = trim(right_side) - apply_operator(pad_z(second), trim(second), weights, diagonal)
    return (trim(second), residual)


def collect_grid(right_side, coefficient):
    sx, sy, sz = right_side.shape
    count_x = lax.axis_size("xb")
    count_y = lax.axis_size("yb")
    flat = jnp.concatenate([right_side.reshape(1, -1), coefficient.reshape(1, -1)], axis=1)
    both = lax.all_gather(flat, ("xb", "yb"), axis=0, tiled=True)
    size = sx * sy * sz
    return tuple(
        (
            piece.reshape(count_x, count_y, sx, sy, sz)
            .transpose(0, 2, 1, 3, 4)
            .reshape(count_x * sx, count_y * sy, sz)
            for piece in (both[:, :size], both[:, size:])
        )
    )


def own_block(whole, shape):
    start_x = lax.axis_index("xb") * shape[0]
    start_y = lax.axis_index("yb") * shape[1]
    return lax.dynamic_slice(whole, (start_x, start_y, jnp.int32(0)), shape)


def per_device(initial_guess, right_side, coefficient):
    mid_coef = restrict_field(coefficient)
    low_coef = restrict_field(mid_coef)
    low_size = low_coef.shape[0]
    low_first = min(3, low_size)
    assert low_first == 3 or 2 * low_size >= 3
    guess_b, rhs_b, coef_b, mid_coef_b, low_coef_b = exchange_once(
        [(initial_guess, 3, 7), (right_side, 2, 7), (coefficient, 3, 7)],
        [(mid_coef, 3), (low_coef, 3)],
    )
    fine, fine_res = smooth_box(guess_b, rhs_b[:, 1:-1], coef_b, 1.0)
    fine = fine[:, 4:-4]
    mid_rhs = restrict_field(fine_res)
    mid_rhs_b, mid_coef_b, low_coef_b = exchange(
        [(mid_rhs, 2), (mid_coef_b, 3), (low_coef_b, low_first)], "xb", 0
    )[0]
    middle, mid_res = smooth_box(None, mid_rhs_b, mid_coef_b, 0.25)
    low_rhs = restrict_field(mid_res)
    forwards = ()
    if low_first < 3:
        forwards = ((low_coef_b, (2 * low_size - 3, low_size), (2 * low_size, low_size + 3)),)
    boxes = exchange_once([(low_rhs, 2, 2)], (), forwards)
    low_rhs_b = boxes[0]
    if low_first < 3:
        low_coef_b = boxes[1]
    lower, low_res = smooth_box(None, low_rhs_b, low_coef_b, 0.0625)
    coarse_rhs, coarse_coef = collect_grid(restrict_field(low_res), restrict_field(low_coef))
    coarse_whole = coarse_solve(coarse_rhs, coarse_coef, 0.015625, extend_all)
    sx, sy, sz = right_side.shape
    coarse = own_block(coarse_whole, (sx // 8, sy // 8, sz // 8))
    return (fine, middle, lower, coarse)


def solution(mesh):
    placed = (P("xb", "yb", None), P("xb", "yb", None), P("xb", "yb", None))
    return jax.shard_map(
        per_device,
        mesh=mesh,
        in_specs=placed,
        out_specs=(
            P("xb", "yb", None),
            P("xb", "yb", None),
            P("xb", "yb", None),
            P("xb", "yb", None),
        ),
        check_vma=False,
    )
```

```python
import jax
import jax.numpy as jnp
from jax import lax
from jax.sharding import PartitionSpec as P


COARSE_ITERS = 8


damping_alpha = 0.05
cheb_theta = 1.15
cheb_delta = 0.85
cheb_sigma = cheb_theta / cheb_delta
cheb_first = 1.0 / cheb_sigma
cheb_second = 1.0 / (2.0 * cheb_sigma - cheb_first)
cheb_carry = cheb_second * cheb_first
cheb_resid = 2.0 * cheb_second / cheb_delta
jacobi_weight = 0.8


def exchange(items, axis, dim, forwards=()):
    count = lax.axis_size(axis)
    low = [[] for _ in items]
    high = [[] for _ in items]
    boxes = [box for box, _, _ in forwards]
    reach = max(-(-width // block.shape[dim]) for block, width in items)
    for hop in range(1, reach + 1):
        for sign in (1, -1):
            pieces = []
            owners = []
            for index, (block, width) in enumerate(items):
                size = block.shape[dim]
                rows = min(size, width - (hop - 1) * size)
                if rows <= 0:
                    continue
                begin = size - rows if sign == 1 else 0
                pieces.append(lax.slice_in_dim(block, begin, begin + rows, axis=dim))
                owners.append(index)
            if hop == 1:
                for index, (box, rows_low, rows_high) in enumerate(forwards):
                    rows = rows_low if sign == 1 else rows_high
                    pieces.append(lax.slice_in_dim(box, rows[0], rows[1], axis=dim))
                    owners.append(-1 - index)
            common = [max(p.shape[d] for p in pieces) for d in (1, 2)]
            joined = jnp.concatenate(
                [
                    jnp.pad(p, ((0, 0), (0, common[0] - p.shape[1]), (0, common[1] - p.shape[2])))
                    for p in pieces
                ],
                axis=0,
            )
            if sign == 1:
                pairs = [(i, i + hop) for i in range(count - hop)]
            else:
                pairs = [(i + hop, i) for i in range(count - hop)]
            got = lax.ppermute(joined, axis, pairs)
            offset = 0
            for index, piece in zip(owners, pieces):
                part = got[offset : offset + piece.shape[0], : piece.shape[1], : piece.shape[2]]
                offset += piece.shape[0]
                if index < 0:
                    box = boxes[-1 - index]
                    parts = [part, box] if sign == 1 else [box, part]
                    boxes[-1 - index] = jnp.concatenate(parts, axis=dim)
                elif sign == 1:
                    low[index].insert(0, part)
                else:
                    high[index].append(part)
    extended = [
        jnp.concatenate(low[i] + [block] + high[i], axis=dim)
        for i, (block, width) in enumerate(items)
    ]
    return extended, boxes


def send(pieces, axis, pairs):
    common = [max(p.shape[d] for p in pieces) for d in (1, 2)]
    joined = jnp.concatenate(
        [
            jnp.pad(p, ((0, 0), (0, common[0] - p.shape[1]), (0, common[1] - p.shape[2])))
            for p in pieces
        ],
        axis=0,
    )
    got = lax.ppermute(joined, axis, pairs)
    parts = []
    offset = 0
    for piece in pieces:
        parts.append(got[offset : offset + piece.shape[0], : piece.shape[1], : piece.shape[2]])
        offset += piece.shape[0]
    return parts


def exchange_once(items, extras):
    count_x = lax.axis_size("xb")
    count_y = lax.axis_size("yb")
    boxes = []
    faces = {}
    for sign in (1, -1):
        pairs = [(i, i + 1) for i in range(count_x - 1)]
        if sign == -1:
            pairs = [(j, i) for i, j in pairs]
        pieces = []
        for block, wx, wy in items:
            size = block.shape[0]
            begin = size - wx if sign == 1 else 0
            pieces.append(block[begin : begin + wx])
        faces[("x", sign)] = send(pieces, "xb", pairs)
    for sign in (1, -1):
        pairs = [(i, i + 1) for i in range(count_y - 1)]
        if sign == -1:
            pairs = [(j, i) for i, j in pairs]
        pieces = []
        for block, _, wy in list(items) + [(b, 0, w) for b, w in extras]:
            size = block.shape[1]
            begin = size - wy if sign == 1 else 0
            pieces.append(block[:, begin : begin + wy])
        faces[("y", sign)] = send(pieces, "yb", pairs)
    for sx in (1, -1):
        for sy in (1, -1):
            pairs = []
            for a in range(count_x):
                for b in range(count_y):
                    if 0 <= a + sx < count_x and 0 <= b + sy < count_y:
                        pairs.append((a * count_y + b, (a + sx) * count_y + (b + sy)))
            pieces = []
            for block, wx, wy in items:
                bx, by = block.shape[0], block.shape[1]
                x0 = bx - wx if sx == 1 else 0
                y0 = by - wy if sy == 1 else 0
                pieces.append(block[x0 : x0 + wx, y0 : y0 + wy])
            faces[(sx, sy)] = send(pieces, ("xb", "yb"), pairs)
    for index, (block, wx, wy) in enumerate(items):
        low = jnp.concatenate(
            [faces[(1, 1)][index], faces[("x", 1)][index], faces[(1, -1)][index]], axis=1
        )
        middle = jnp.concatenate(
            [faces[("y", 1)][index], block, faces[("y", -1)][index]], axis=1
        )
        high = jnp.concatenate(
            [faces[(-1, 1)][index], faces[("x", -1)][index], faces[(-1, -1)][index]], axis=1
        )
        boxes.append(jnp.concatenate([low, middle, high], axis=0))
    for index, (block, wy) in enumerate(extras):
        index += len(items)
        boxes.append(
            jnp.concatenate([faces[("y", 1)][index], block, faces[("y", -1)][index]], axis=1)
        )
    return boxes


def pad_z(box):
    return jnp.pad(box, ((0, 0), (0, 0), (1, 1)))


def trim(box):
    return box[1:-1, 1:-1, :]


def neighbours(padded):
    return [
        padded[2:, 1:-1, 1:-1],
        padded[:-2, 1:-1, 1:-1],
        padded[1:-1, 2:, 1:-1],
        padded[1:-1, :-2, 1:-1],
        padded[1:-1, 1:-1, 2:],
        padded[1:-1, 1:-1, :-2],
    ]


def face_weights(padded_coef, scale):
    centre = padded_coef[1:-1, 1:-1, 1:-1]
    weights = [0.5 * scale * (centre + other) for other in neighbours(padded_coef)]
    diagonal = damping_alpha + weights[0]
    for other in weights[1:]:
        diagonal = diagonal + other
    return (weights, diagonal)


def apply_operator(padded, field, weights, diagonal):
    result = diagonal * field
    for weight, other in zip(weights, neighbours(padded)):
        result = result - weight * other
    return result


def pair_matrix(count):
    rows = jnp.arange(count // 2)[:, None]
    cols = jnp.arange(count)[None, :] // 2
    return (rows == cols).astype(jnp.float32)


def restrict_field(field):
    sx, sy, sz = field.shape
    halves = field.reshape(sx // 2, 2, sy, sz)
    summed = halves[:, 0] + halves[:, 1]
    summed = jnp.einsum(
        "xyZ,zZ->xyz", summed, pair_matrix(sz), precision=lax.Precision.HIGHEST
    )
    pairs_y = jnp.broadcast_to(pair_matrix(sy), (sx // 2, sy // 2, sy))
    summed = jnp.einsum(
        "xyY,xYz->xyz", pairs_y, summed, precision=lax.Precision.HIGHEST
    )
    return summed * 0.125


def coarse_solve(right_side, coefficient, scale, extend):
    weights, diagonal = face_weights(extend(coefficient), scale)
    field = jnp.zeros_like(right_side)
    for _ in range(COARSE_ITERS):
        field = (
            field
            + jacobi_weight
            * (right_side - apply_operator(extend(field), field, weights, diagonal))
            / diagonal
        )
    leftover = right_side - apply_operator(extend(field), field, weights, diagonal)
    ones_field = jnp.ones_like(right_side)
    image_ones = apply_operator(extend(ones_field), ones_field, weights, diagonal)
    return field + jnp.sum(leftover) / jnp.sum(image_ones)


def extend_all(field):
    return jnp.pad(field, 1)


def box_weights(padded_coef, scale):
    centre = padded_coef[1:-1, 1:-1, 1:-1]
    outside = centre == 0.0
    weights = [
        jnp.where(outside, 0.0, 0.5 * scale * (centre + other))
        for other in neighbours(padded_coef)
    ]
    diagonal = damping_alpha + weights[0]
    for other in weights[1:]:
        diagonal = diagonal + other
    return (weights, diagonal)


def smooth_box(start, right_side, coefficient, scale):
    weights, diagonal = box_weights(pad_z(coefficient), scale)
    if start is None:
        start = jnp.zeros_like(right_side)
        residual = right_side
    else:
        residual = right_side - apply_operator(pad_z(start), trim(start), weights, diagonal)
        start = trim(start)
    first_step = residual / (cheb_theta * diagonal)
    first = start + first_step
    weights = [trim(w) for w in weights]
    diagonal = trim(diagonal)
    right_side = trim(right_side)
    residual = right_side - apply_operator(pad_z(first), trim(first), weights, diagonal)
    second_step = cheb_carry * trim(first_step) + cheb_resid * residual / diagonal
    second = trim(first) + second_step
    weights = [trim(w) for w in weights]
    diagonal = trim(diagonal)
    residual = trim(right_side) - apply_operator(pad_z(second), trim(second), weights, diagonal)
    return (trim(second), residual)


def collect_grid(right_side, coefficient):
    sx, sy, sz = right_side.shape
    count_x = lax.axis_size("xb")
    count_y = lax.axis_size("yb")
    flat = jnp.concatenate([right_side.reshape(1, -1), coefficient.reshape(1, -1)], axis=1)
    both = lax.all_to_all(
        jnp.broadcast_to(flat, (count_x * count_y, flat.shape[1])), ("xb", "yb"), 0, 0, tiled=True
    )
    size = sx * sy * sz
    return tuple(
        (
            piece.reshape(count_x, count_y, sx, sy, sz)
            .transpose(0, 2, 1, 3, 4)
            .reshape(count_x * sx, count_y * sy, sz)
            for piece in (both[:, :size], both[:, size:])
        )
    )


def own_block(whole, shape):
    start_x = lax.axis_index("xb") * shape[0]
    start_y = lax.axis_index("yb") * shape[1]
    return lax.dynamic_slice(whole, (start_x, start_y, jnp.int32(0)), shape)


def per_device(initial_guess, right_side, coefficient):
    mid_coef = restrict_field(coefficient)
    low_coef = restrict_field(mid_coef)
    low_size = low_coef.shape[0]
    low_first = min(3, low_size)
    assert low_first == 3 or 2 * low_size >= 3
    guess_b, rhs_b, coef_b, mid_coef_b, low_coef_b = exchange_once(
        [(initial_guess, 3, 7), (right_side, 2, 7), (coefficient, 3, 7)],
        [(mid_coef, 3), (low_coef, 3)],
    )
    fine, fine_res = smooth_box(guess_b, rhs_b[:, 1:-1], coef_b, 1.0)
    fine = fine[:, 4:-4]
    mid_rhs = restrict_field(fine_res)
    mid_rhs_b, mid_coef_b, low_coef_b = exchange(
        [(mid_rhs, 2), (mid_coef_b, 3), (low_coef_b, low_first)], "xb", 0
    )[0]
    middle, mid_res = smooth_box(None, mid_rhs_b, mid_coef_b, 0.25)
    low_rhs = restrict_field(mid_res)
    (low_rhs_b,) = exchange([(low_rhs, 3)], "yb", 1)[0]
    forwards = ()
    if low_first < 3:
        forwards = ((low_coef_b, (2 * low_size - 3, low_size), (2 * low_size, low_size + 3)),)
    (low_rhs_b,), boxes = exchange([(low_rhs_b, 2)], "xb", 0, forwards)
    if low_first < 3:
        (low_coef_b,) = boxes
    lower, low_res = smooth_box(None, low_rhs_b[:, 1:-1], low_coef_b, 0.0625)
    coarse_rhs, coarse_coef = collect_grid(restrict_field(low_res), restrict_field(low_coef))
    coarse_whole = coarse_solve(coarse_rhs, coarse_coef, 0.015625, extend_all)
    sx, sy, sz = right_side.shape
    coarse = own_block(coarse_whole, (sx // 8, sy // 8, sz // 8))
    return (fine, middle, lower, coarse)


def solution(mesh):
    placed = (P("xb", "yb", None), P("xb", "yb", None), P("xb", "yb", None))
    return jax.shard_map(
        per_device,
        mesh=mesh,
        in_specs=placed,
        out_specs=(
            P("xb", "yb", None),
            P("xb", "yb", None),
            P("xb", "yb", None),
            P("xb", "yb", None),
        ),
        check_vma=False,
    )
```

```python
import jax
import jax.numpy as jnp
from jax import lax
from jax.sharding import PartitionSpec as P


COARSE_ITERS = 8


damping_alpha = 0.05
cheb_theta = 1.15
cheb_delta = 0.85
cheb_sigma = cheb_theta / cheb_delta
cheb_first = 1.0 / cheb_sigma
cheb_second = 1.0 / (2.0 * cheb_sigma - cheb_first)
cheb_carry = cheb_second * cheb_first
cheb_resid = 2.0 * cheb_second / cheb_delta
jacobi_weight = 0.8


def exchange(items, axis, dim, forwards=()):
    count = lax.axis_size(axis)
    low = [[] for _ in items]
    high = [[] for _ in items]
    boxes = [box for box, _, _ in forwards]
    reach = max(-(-width // block.shape[dim]) for block, width in items)
    for hop in range(1, reach + 1):
        for sign in (1, -1):
            pieces = []
            owners = []
            for index, (block, width) in enumerate(items):
                size = block.shape[dim]
                rows = min(size, width - (hop - 1) * size)
                if rows <= 0:
                    continue
                begin = size - rows if sign == 1 else 0
                pieces.append(lax.slice_in_dim(block, begin, begin + rows, axis=dim))
                owners.append(index)
            if hop == 1:
                for index, (box, rows_low, rows_high) in enumerate(forwards):
                    rows = rows_low if sign == 1 else rows_high
                    pieces.append(lax.slice_in_dim(box, rows[0], rows[1], axis=dim))
                    owners.append(-1 - index)
            common = [max(p.shape[d] for p in pieces) for d in (1, 2)]
            joined = jnp.concatenate(
                [
                    jnp.pad(p, ((0, 0), (0, common[0] - p.shape[1]), (0, common[1] - p.shape[2])))
                    for p in pieces
                ],
                axis=0,
            )
            if sign == 1:
                pairs = [(i, i + hop) for i in range(count - hop)]
            else:
                pairs = [(i + hop, i) for i in range(count - hop)]
            got = lax.ppermute(joined, axis, pairs)
            offset = 0
            for index, piece in zip(owners, pieces):
                part = got[offset : offset + piece.shape[0], : piece.shape[1], : piece.shape[2]]
                offset += piece.shape[0]
                if index < 0:
                    box = boxes[-1 - index]
                    parts = [part, box] if sign == 1 else [box, part]
                    boxes[-1 - index] = jnp.concatenate(parts, axis=dim)
                elif sign == 1:
                    low[index].insert(0, part)
                else:
                    high[index].append(part)
    extended = [
        jnp.concatenate(low[i] + [block] + high[i], axis=dim)
        for i, (block, width) in enumerate(items)
    ]
    return extended, boxes


def send(pieces, axis, pairs):
    common = [max(p.shape[d] for p in pieces) for d in (1, 2)]
    joined = jnp.concatenate(
        [
            jnp.pad(p, ((0, 0), (0, common[0] - p.shape[1]), (0, common[1] - p.shape[2])))
            for p in pieces
        ],
        axis=0,
    )
    got = lax.ppermute(joined, axis, pairs)
    parts = []
    offset = 0
    for piece in pieces:
        parts.append(got[offset : offset + piece.shape[0], : piece.shape[1], : piece.shape[2]])
        offset += piece.shape[0]
    return parts


def exchange_once(items, extras):
    count_x = lax.axis_size("xb")
    count_y = lax.axis_size("yb")
    boxes = []
    faces = {}
    for sign in (1, -1):
        pairs = [(i, i + 1) for i in range(count_x - 1)]
        if sign == -1:
            pairs = [(j, i) for i, j in pairs]
        pieces = []
        for block, wx, wy in items:
            size = block.shape[0]
            begin = size - wx if sign == 1 else 0
            pieces.append(block[begin : begin + wx])
        faces[("x", sign)] = send(pieces, "xb", pairs)
    for sign in (1, -1):
        pairs = [(i, i + 1) for i in range(count_y - 1)]
        if sign == -1:
            pairs = [(j, i) for i, j in pairs]
        pieces = []
        for block, _, wy in list(items) + [(b, 0, w) for b, w in extras]:
            size = block.shape[1]
            begin = size - wy if sign == 1 else 0
            pieces.append(block[:, begin : begin + wy])
        faces[("y", sign)] = send(pieces, "yb", pairs)
    for sx in (1, -1):
        for sy in (1, -1):
            pairs = []
            for a in range(count_x):
                for b in range(count_y):
                    if 0 <= a + sx < count_x and 0 <= b + sy < count_y:
                        pairs.append((a * count_y + b, (a + sx) * count_y + (b + sy)))
            pieces = []
            for block, wx, wy in items:
                bx, by = block.shape[0], block.shape[1]
                x0 = bx - wx if sx == 1 else 0
                y0 = by - wy if sy == 1 else 0
                pieces.append(block[x0 : x0 + wx, y0 : y0 + wy])
            faces[(sx, sy)] = send(pieces, ("xb", "yb"), pairs)
    for index, (block, wx, wy) in enumerate(items):
        low = jnp.concatenate(
            [faces[(1, 1)][index], faces[("x", 1)][index], faces[(1, -1)][index]], axis=1
        )
        middle = jnp.concatenate(
            [faces[("y", 1)][index], block, faces[("y", -1)][index]], axis=1
        )
        high = jnp.concatenate(
            [faces[(-1, 1)][index], faces[("x", -1)][index], faces[(-1, -1)][index]], axis=1
        )
        boxes.append(jnp.concatenate([low, middle, high], axis=0))
    for index, (block, wy) in enumerate(extras):
        index += len(items)
        boxes.append(
            jnp.concatenate([faces[("y", 1)][index], block, faces[("y", -1)][index]], axis=1)
        )
    return boxes


def pad_z(box):
    return jnp.pad(box, ((0, 0), (0, 0), (1, 1)))


def trim(box):
    return box[1:-1, 1:-1, :]


def neighbours(padded):
    return [
        padded[2:, 1:-1, 1:-1],
        padded[:-2, 1:-1, 1:-1],
        padded[1:-1, 2:, 1:-1],
        padded[1:-1, :-2, 1:-1],
        padded[1:-1, 1:-1, 2:],
        padded[1:-1, 1:-1, :-2],
    ]


def face_weights(padded_coef, scale):
    centre = padded_coef[1:-1, 1:-1, 1:-1]
    weights = [0.5 * scale * (centre + other) for other in neighbours(padded_coef)]
    diagonal = damping_alpha + weights[0]
    for other in weights[1:]:
        diagonal = diagonal + other
    return (weights, diagonal)


def apply_operator(padded, field, weights, diagonal):
    result = diagonal * field
    for weight, other in zip(weights, neighbours(padded)):
        result = result - weight * other
    return result


def pair_matrix(count):
    rows = jnp.arange(count // 2)[:, None]
    cols = jnp.arange(count)[None, :] // 2
    return (rows == cols).astype(jnp.float32)


def restrict_field(field):
    sx, sy, sz = field.shape
    halves = field.reshape(sx // 2, 2, sy, sz)
    summed = halves[:, 0] + halves[:, 1]
    summed = jnp.einsum(
        "xyZ,zZ->xyz", summed, pair_matrix(sz), precision=lax.Precision.HIGHEST
    )
    pairs_y = jnp.broadcast_to(pair_matrix(sy), (sx // 2, sy // 2, sy))
    summed = jnp.einsum(
        "xyY,xYz->xyz", pairs_y, summed, precision=lax.Precision.HIGHEST
    )
    return summed * 0.125


def coarse_solve(right_side, coefficient, scale, extend):
    weights, diagonal = face_weights(extend(coefficient), scale)
    field = jnp.zeros_like(right_side)
    for _ in range(COARSE_ITERS):
        field = (
            field
            + jacobi_weight
            * (right_side - apply_operator(extend(field), field, weights, diagonal))
            / diagonal
        )
    leftover = right_side - apply_operator(extend(field), field, weights, diagonal)
    ones_field = jnp.ones_like(right_side)
    image_ones = apply_operator(extend(ones_field), ones_field, weights, diagonal)
    return field + jnp.sum(leftover) / jnp.sum(image_ones)


def extend_all(field):
    return jnp.pad(field, 1)


def box_weights(padded_coef, scale):
    centre = padded_coef[1:-1, 1:-1, 1:-1]
    outside = centre == 0.0
    weights = [
        jnp.where(outside, 0.0, 0.5 * scale * (centre + other))
        for other in neighbours(padded_coef)
    ]
    diagonal = damping_alpha + weights[0]
    for other in weights[1:]:
        diagonal = diagonal + other
    return (weights, diagonal)


def smooth_box(start, right_side, coefficient, scale):
    weights, diagonal = box_weights(pad_z(coefficient), scale)
    if start is None:
        start = jnp.zeros_like(right_side)
        residual = right_side
    else:
        residual = right_side - apply_operator(pad_z(start), trim(start), weights, diagonal)
        start = trim(start)
    first_step = residual / (cheb_theta * diagonal)
    first = start + first_step
    weights = [trim(w) for w in weights]
    diagonal = trim(diagonal)
    right_side = trim(right_side)
    residual = right_side - apply_operator(pad_z(first), trim(first), weights, diagonal)
    second_step = cheb_carry * trim(first_step) + cheb_resid * residual / diagonal
    second = trim(first) + second_step
    weights = [trim(w) for w in weights]
    diagonal = trim(diagonal)
    residual = trim(right_side) - apply_operator(pad_z(second), trim(second), weights, diagonal)
    return (trim(second), residual)


def collect_grid(block):
    sx, sy, sz = block.shape
    count_x = lax.axis_size("xb")
    count_y = lax.axis_size("yb")
    flat = block.reshape(1, -1)
    every = lax.all_to_all(
        jnp.broadcast_to(flat, (count_x * count_y, flat.shape[1])), ("xb", "yb"), 0, 0, tiled=True
    )
    return (
        every.reshape(count_x, count_y, sx, sy, sz)
        .transpose(0, 2, 1, 3, 4)
        .reshape(count_x * sx, count_y * sy, sz)
    )


def own_block(whole, shape):
    start_x = lax.axis_index("xb") * shape[0]
    start_y = lax.axis_index("yb") * shape[1]
    return lax.dynamic_slice(whole, (start_x, start_y, jnp.int32(0)), shape)


def per_device(initial_guess, right_side, coefficient):
    mid_coef = restrict_field(coefficient)
    low_coef = restrict_field(mid_coef)
    coarse_coef = collect_grid(restrict_field(low_coef))
    low_size = low_coef.shape[0]
    low_first = min(3, low_size)
    assert low_first == 3 or 2 * low_size >= 3
    guess_b, rhs_b, coef_b, mid_coef_b, low_coef_b = exchange_once(
        [(initial_guess, 3, 7), (right_side, 2, 7), (coefficient, 3, 7)],
        [(mid_coef, 3), (low_coef, 3)],
    )
    fine, fine_res = smooth_box(guess_b, rhs_b[:, 1:-1], coef_b, 1.0)
    fine = fine[:, 4:-4]
    mid_rhs = restrict_field(fine_res)
    mid_rhs_b, mid_coef_b, low_coef_b = exchange(
        [(mid_rhs, 2), (mid_coef_b, 3), (low_coef_b, low_first)], "xb", 0
    )[0]
    middle, mid_res = smooth_box(None, mid_rhs_b, mid_coef_b, 0.25)
    low_rhs = restrict_field(mid_res)
    (low_rhs_b,) = exchange([(low_rhs, 3)], "yb", 1)[0]
    forwards = ()
    if low_first < 3:
        forwards = ((low_coef_b, (2 * low_size - 3, low_size), (2 * low_size, low_size + 3)),)
    (low_rhs_b,), boxes = exchange([(low_rhs_b, 2)], "xb", 0, forwards)
    if low_first < 3:
        (low_coef_b,) = boxes
    lower, low_res = smooth_box(None, low_rhs_b[:, 1:-1], low_coef_b, 0.0625)
    coarse_rhs = collect_grid(restrict_field(low_res))
    coarse_whole = coarse_solve(coarse_rhs, coarse_coef, 0.015625, extend_all)
    sx, sy, sz = right_side.shape
    coarse = own_block(coarse_whole, (sx // 8, sy // 8, sz // 8))
    return (fine, middle, lower, coarse)


def solution(mesh):
    placed = (P("xb", "yb", None), P("xb", "yb", None), P("xb", "yb", None))
    return jax.shard_map(
        per_device,
        mesh=mesh,
        in_specs=placed,
        out_specs=(
            P("xb", "yb", None),
            P("xb", "yb", None),
            P("xb", "yb", None),
            P("xb", "yb", None),
        ),
        check_vma=False,
    )
```

```python
import jax
import jax.numpy as jnp
from jax import lax
from jax.experimental import pallas as pl
from jax.experimental.pallas import tpu as pltpu
from jax.sharding import PartitionSpec as P


COARSE_ITERS = 8


damping_alpha = 0.05
cheb_theta = 1.15
cheb_delta = 0.85
cheb_sigma = cheb_theta / cheb_delta
cheb_first = 1.0 / cheb_sigma
cheb_second = 1.0 / (2.0 * cheb_sigma - cheb_first)
cheb_carry = cheb_second * cheb_first
cheb_resid = 2.0 * cheb_second / cheb_delta
jacobi_weight = 0.8


def exchange(items, axis, dim, forwards=()):
    count = lax.axis_size(axis)
    low = [[] for _ in items]
    high = [[] for _ in items]
    boxes = [box for box, _, _ in forwards]
    reach = max(-(-width // block.shape[dim]) for block, width in items)
    for hop in range(1, reach + 1):
        for sign in (1, -1):
            pieces = []
            owners = []
            for index, (block, width) in enumerate(items):
                size = block.shape[dim]
                rows = min(size, width - (hop - 1) * size)
                if rows <= 0:
                    continue
                begin = size - rows if sign == 1 else 0
                pieces.append(lax.slice_in_dim(block, begin, begin + rows, axis=dim))
                owners.append(index)
            if hop == 1:
                for index, (box, rows_low, rows_high) in enumerate(forwards):
                    rows = rows_low if sign == 1 else rows_high
                    pieces.append(lax.slice_in_dim(box, rows[0], rows[1], axis=dim))
                    owners.append(-1 - index)
            common = [max(p.shape[d] for p in pieces) for d in (1, 2)]
            joined = jnp.concatenate(
                [
                    jnp.pad(p, ((0, 0), (0, common[0] - p.shape[1]), (0, common[1] - p.shape[2])))
                    for p in pieces
                ],
                axis=0,
            )
            if sign == 1:
                pairs = [(i, i + hop) for i in range(count - hop)]
            else:
                pairs = [(i + hop, i) for i in range(count - hop)]
            got = lax.ppermute(joined, axis, pairs)
            offset = 0
            for index, piece in zip(owners, pieces):
                part = got[offset : offset + piece.shape[0], : piece.shape[1], : piece.shape[2]]
                offset += piece.shape[0]
                if index < 0:
                    box = boxes[-1 - index]
                    parts = [part, box] if sign == 1 else [box, part]
                    boxes[-1 - index] = jnp.concatenate(parts, axis=dim)
                elif sign == 1:
                    low[index].insert(0, part)
                else:
                    high[index].append(part)
    extended = [
        jnp.concatenate(low[i] + [block] + high[i], axis=dim)
        for i, (block, width) in enumerate(items)
    ]
    return extended, boxes


def send(pieces, axis, pairs):
    common = [max(p.shape[d] for p in pieces) for d in (1, 2)]
    joined = jnp.concatenate(
        [
            jnp.pad(p, ((0, 0), (0, common[0] - p.shape[1]), (0, common[1] - p.shape[2])))
            for p in pieces
        ],
        axis=0,
    )
    got = lax.ppermute(joined, axis, pairs)
    parts = []
    offset = 0
    for piece in pieces:
        parts.append(got[offset : offset + piece.shape[0], : piece.shape[1], : piece.shape[2]])
        offset += piece.shape[0]
    return parts


def exchange_once(items, extras):
    count_x = lax.axis_size("xb")
    count_y = lax.axis_size("yb")
    boxes = []
    faces = {}
    for sign in (1, -1):
        pairs = [(i, i + 1) for i in range(count_x - 1)]
        if sign == -1:
            pairs = [(j, i) for i, j in pairs]
        pieces = []
        for block, wx, wy in items:
            size = block.shape[0]
            begin = size - wx if sign == 1 else 0
            pieces.append(block[begin : begin + wx])
        faces[("x", sign)] = send(pieces, "xb", pairs)
    for sign in (1, -1):
        pairs = [(i, i + 1) for i in range(count_y - 1)]
        if sign == -1:
            pairs = [(j, i) for i, j in pairs]
        pieces = []
        for block, _, wy in list(items) + [(b, 0, w) for b, w in extras]:
            size = block.shape[1]
            begin = size - wy if sign == 1 else 0
            pieces.append(block[:, begin : begin + wy])
        faces[("y", sign)] = send(pieces, "yb", pairs)
    for sx in (1, -1):
        for sy in (1, -1):
            pairs = []
            for a in range(count_x):
                for b in range(count_y):
                    if 0 <= a + sx < count_x and 0 <= b + sy < count_y:
                        pairs.append((a * count_y + b, (a + sx) * count_y + (b + sy)))
            pieces = []
            for block, wx, wy in items:
                bx, by = block.shape[0], block.shape[1]
                x0 = bx - wx if sx == 1 else 0
                y0 = by - wy if sy == 1 else 0
                pieces.append(block[x0 : x0 + wx, y0 : y0 + wy])
            faces[(sx, sy)] = send(pieces, ("xb", "yb"), pairs)
    for index, (block, wx, wy) in enumerate(items):
        low = jnp.concatenate(
            [faces[(1, 1)][index], faces[("x", 1)][index], faces[(1, -1)][index]], axis=1
        )
        middle = jnp.concatenate(
            [faces[("y", 1)][index], block, faces[("y", -1)][index]], axis=1
        )
        high = jnp.concatenate(
            [faces[(-1, 1)][index], faces[("x", -1)][index], faces[(-1, -1)][index]], axis=1
        )
        boxes.append(jnp.concatenate([low, middle, high], axis=0))
    for index, (block, wy) in enumerate(extras):
        index += len(items)
        boxes.append(
            jnp.concatenate([faces[("y", 1)][index], block, faces[("y", -1)][index]], axis=1)
        )
    return boxes


def pad_z(box):
    return jnp.pad(box, ((0, 0), (0, 0), (1, 1)))


def trim(box):
    return box[1:-1, 1:-1, :]


def neighbours(padded):
    return [
        padded[2:, 1:-1, 1:-1],
        padded[:-2, 1:-1, 1:-1],
        padded[1:-1, 2:, 1:-1],
        padded[1:-1, :-2, 1:-1],
        padded[1:-1, 1:-1, 2:],
        padded[1:-1, 1:-1, :-2],
    ]


def apply_operator(padded, field, weights, diagonal):
    result = diagonal * field
    for weight, other in zip(weights, neighbours(padded)):
        result = result - weight * other
    return result


def pair_matrix(count):
    rows = jnp.arange(count // 2)[:, None]
    cols = jnp.arange(count)[None, :] // 2
    return (rows == cols).astype(jnp.float32)


def restrict_field(field):
    sx, sy, sz = field.shape
    halves = field.reshape(sx // 2, 2, sy, sz)
    summed = halves[:, 0] + halves[:, 1]
    summed = jnp.einsum(
        "xyZ,zZ->xyz", summed, pair_matrix(sz), precision=lax.Precision.HIGHEST
    )
    pairs_y = jnp.broadcast_to(pair_matrix(sy), (sx // 2, sy // 2, sy))
    summed = jnp.einsum(
        "xyY,xYz->xyz", pairs_y, summed, precision=lax.Precision.HIGHEST
    )
    return summed * 0.125


def box_weights(padded_coef, scale):
    centre = padded_coef[1:-1, 1:-1, 1:-1]
    outside = centre == 0.0
    weights = [
        jnp.where(outside, 0.0, 0.5 * scale * (centre + other))
        for other in neighbours(padded_coef)
    ]
    diagonal = damping_alpha + weights[0]
    for other in weights[1:]:
        diagonal = diagonal + other
    return (weights, diagonal)


def smooth_box(start, right_side, coefficient, scale):
    weights, diagonal = box_weights(pad_z(coefficient), scale)
    if start is None:
        start = jnp.zeros_like(right_side)
        residual = right_side
    else:
        residual = right_side - apply_operator(pad_z(start), trim(start), weights, diagonal)
        start = trim(start)
    first_step = residual / (cheb_theta * diagonal)
    first = start + first_step
    weights = [trim(w) for w in weights]
    diagonal = trim(diagonal)
    right_side = trim(right_side)
    residual = right_side - apply_operator(pad_z(first), trim(first), weights, diagonal)
    second_step = cheb_carry * trim(first_step) + cheb_resid * residual / diagonal
    second = trim(first) + second_step
    weights = [trim(w) for w in weights]
    diagonal = trim(diagonal)
    residual = trim(right_side) - apply_operator(pad_z(second), trim(second), weights, diagonal)
    return (trim(second), residual)


def collect_grid(right_side, coefficient):
    sx, sy, sz = right_side.shape
    count_x = lax.axis_size("xb")
    count_y = lax.axis_size("yb")
    flat = jnp.concatenate([right_side.reshape(1, -1), coefficient.reshape(1, -1)], axis=1)
    both = lax.all_to_all(
        jnp.broadcast_to(flat, (count_x * count_y, flat.shape[1])), ("xb", "yb"), 0, 0, tiled=True
    )
    size = sx * sy * sz
    return tuple(
        (
            piece.reshape(count_x, count_y, sx, sy, sz)
            .transpose(0, 2, 1, 3, 4)
            .reshape(count_x * sx, count_y * sy, sz)
            for piece in (both[:, :size], both[:, size:])
        )
    )


def coarse_kernel_body(scale, nx, ny, nz, iters):
    def body(rhs_ref, coef_ref, out_ref):
        f = rhs_ref[...]
        k = coef_ref[...]
        width = ny * nz
        row = jax.lax.broadcasted_iota(jnp.int32, (nx, width), 0)
        lane = jax.lax.broadcasted_iota(jnp.int32, (nx, width), 1)
        zpos = lane % nz
        masks = [row < nx - 1, row > 0, lane < width - nz, lane >= nz, zpos < nz - 1, zpos > 0]
        shifts = [(nx - 1, 0), (1, 0), (width - nz, 1), (nz, 1), (width - 1, 1), (1, 1)]
        def nbs(a):
            return [jnp.where(m, pltpu.roll(a, s, ax), 0.0) for m, (s, ax) in zip(masks, shifts)]
        weights = [(0.5 * scale) * (k + other) for other in nbs(k)]
        diagonal = damping_alpha + weights[0]
        for other in weights[1:]:
            diagonal = diagonal + other
        def apply(v):
            result = diagonal * v
            for w, other in zip(weights, nbs(v)):
                result = result - w * other
            return result
        field = jnp.zeros_like(f)
        for _ in range(iters):
            field = field + jacobi_weight * (f - apply(field)) / diagonal
        leftover = f - apply(field)
        ones = jnp.ones_like(f)
        image = diagonal * ones
        for w, m in zip(weights, masks):
            image = image - w * jnp.where(m, 1.0, 0.0)
        out_ref[...] = field + jnp.sum(leftover) / jnp.sum(image)
    return body


def coarse_pallas(rhs2d, coef2d, scale, ny, nz, iters):
    nx, width = rhs2d.shape
    return pl.pallas_call(
        coarse_kernel_body(scale, nx, ny, nz, iters),
        out_shape=jax.ShapeDtypeStruct((nx, width), jnp.float32),
    )(rhs2d, coef2d)


def per_device(initial_guess, right_side, coefficient):
    mid_coef = restrict_field(coefficient)
    low_coef = restrict_field(mid_coef)
    low_size = low_coef.shape[0]
    low_first = min(3, low_size)
    assert low_first == 3 or 2 * low_size >= 3
    guess_b, rhs_b, coef_b, mid_coef_b, low_coef_b = exchange_once(
        [(initial_guess, 3, 7), (right_side, 2, 7), (coefficient, 3, 7)],
        [(mid_coef, 3), (low_coef, 3)],
    )
    fine, fine_res = smooth_box(guess_b, rhs_b[:, 1:-1], coef_b, 1.0)
    fine = fine[:, 4:-4]
    mid_rhs = restrict_field(fine_res)
    mid_rhs_b, mid_coef_b, low_coef_b = exchange(
        [(mid_rhs, 2), (mid_coef_b, 3), (low_coef_b, low_first)], "xb", 0
    )[0]
    middle, mid_res = smooth_box(None, mid_rhs_b, mid_coef_b, 0.25)
    low_rhs = restrict_field(mid_res)
    (low_rhs_b,) = exchange([(low_rhs, 3)], "yb", 1)[0]
    forwards = ()
    if low_first < 3:
        forwards = ((low_coef_b, (2 * low_size - 3, low_size), (2 * low_size, low_size + 3)),)
    (low_rhs_b,), boxes = exchange([(low_rhs_b, 2)], "xb", 0, forwards)
    if low_first < 3:
        (low_coef_b,) = boxes
    lower, low_res = smooth_box(None, low_rhs_b[:, 1:-1], low_coef_b, 0.0625)
    coarse_rhs, coarse_coef = collect_grid(restrict_field(low_res), restrict_field(low_coef))
    nx, ny, nz = coarse_rhs.shape
    coarse_whole = coarse_pallas(
        coarse_rhs.reshape(nx, ny * nz), coarse_coef.reshape(nx, ny * nz), 0.015625, ny, nz, COARSE_ITERS
    )
    sx, sy, sz = right_side.shape
    sx, sy, sz = sx // 8, sy // 8, sz // 8
    coarse = lax.dynamic_slice(
        coarse_whole,
        (lax.axis_index("xb") * sx, lax.axis_index("yb") * sy * sz),
        (sx, sy * sz),
    ).reshape(sx, sy, sz)
    return (fine, middle, lower, coarse)


def solution(mesh):
    placed = (P("xb", "yb", None), P("xb", "yb", None), P("xb", "yb", None))
    return jax.shard_map(
        per_device,
        mesh=mesh,
        in_specs=placed,
        out_specs=(
            P("xb", "yb", None),
            P("xb", "yb", None),
            P("xb", "yb", None),
            P("xb", "yb", None),
        ),
        check_vma=False,
    )
```

```python
import jax
import jax.numpy as jnp
from jax import lax
from jax.experimental import pallas as pl
from jax.experimental.pallas import tpu as pltpu
from jax.sharding import PartitionSpec as P


COARSE_ITERS = 8


damping_alpha = 0.05
cheb_theta = 1.15
cheb_delta = 0.85
cheb_sigma = cheb_theta / cheb_delta
cheb_first = 1.0 / cheb_sigma
cheb_second = 1.0 / (2.0 * cheb_sigma - cheb_first)
cheb_carry = cheb_second * cheb_first
cheb_resid = 2.0 * cheb_second / cheb_delta
jacobi_weight = 0.8


def exchange(items, axis, dim, forwards=()):
    count = lax.axis_size(axis)
    low = [[] for _ in items]
    high = [[] for _ in items]
    boxes = [box for box, _, _ in forwards]
    reach = max(-(-width // block.shape[dim]) for block, width in items)
    for hop in range(1, reach + 1):
        for sign in (1, -1):
            pieces = []
            owners = []
            for index, (block, width) in enumerate(items):
                size = block.shape[dim]
                rows = min(size, width - (hop - 1) * size)
                if rows <= 0:
                    continue
                begin = size - rows if sign == 1 else 0
                pieces.append(lax.slice_in_dim(block, begin, begin + rows, axis=dim))
                owners.append(index)
            if hop == 1:
                for index, (box, rows_low, rows_high) in enumerate(forwards):
                    rows = rows_low if sign == 1 else rows_high
                    pieces.append(lax.slice_in_dim(box, rows[0], rows[1], axis=dim))
                    owners.append(-1 - index)
            common = [max(p.shape[d] for p in pieces) for d in (1, 2)]
            joined = jnp.concatenate(
                [
                    jnp.pad(p, ((0, 0), (0, common[0] - p.shape[1]), (0, common[1] - p.shape[2])))
                    for p in pieces
                ],
                axis=0,
            )
            if sign == 1:
                pairs = [(i, i + hop) for i in range(count - hop)]
            else:
                pairs = [(i + hop, i) for i in range(count - hop)]
            got = lax.ppermute(joined, axis, pairs)
            offset = 0
            for index, piece in zip(owners, pieces):
                part = got[offset : offset + piece.shape[0], : piece.shape[1], : piece.shape[2]]
                offset += piece.shape[0]
                if index < 0:
                    box = boxes[-1 - index]
                    parts = [part, box] if sign == 1 else [box, part]
                    boxes[-1 - index] = jnp.concatenate(parts, axis=dim)
                elif sign == 1:
                    low[index].insert(0, part)
                else:
                    high[index].append(part)
    extended = [
        jnp.concatenate(low[i] + [block] + high[i], axis=dim)
        for i, (block, width) in enumerate(items)
    ]
    return extended, boxes


def send(pieces, axis, pairs):
    common = [max(p.shape[d] for p in pieces) for d in (1, 2)]
    joined = jnp.concatenate(
        [
            jnp.pad(p, ((0, 0), (0, common[0] - p.shape[1]), (0, common[1] - p.shape[2])))
            for p in pieces
        ],
        axis=0,
    )
    got = lax.ppermute(joined, axis, pairs)
    parts = []
    offset = 0
    for piece in pieces:
        parts.append(got[offset : offset + piece.shape[0], : piece.shape[1], : piece.shape[2]])
        offset += piece.shape[0]
    return parts


def exchange_once(items, extras):
    count_x = lax.axis_size("xb")
    count_y = lax.axis_size("yb")
    boxes = []
    faces = {}
    for sign in (1, -1):
        pairs = [(i, i + 1) for i in range(count_x - 1)]
        if sign == -1:
            pairs = [(j, i) for i, j in pairs]
        pieces = []
        for block, wx, wy in items:
            size = block.shape[0]
            begin = size - wx if sign == 1 else 0
            pieces.append(block[begin : begin + wx])
        faces[("x", sign)] = send(pieces, "xb", pairs)
    for sign in (1, -1):
        pairs = [(i, i + 1) for i in range(count_y - 1)]
        if sign == -1:
            pairs = [(j, i) for i, j in pairs]
        pieces = []
        for block, _, wy in list(items) + [(b, 0, w) for b, w in extras]:
            size = block.shape[1]
            begin = size - wy if sign == 1 else 0
            pieces.append(block[:, begin : begin + wy])
        faces[("y", sign)] = send(pieces, "yb", pairs)
    for sx in (1, -1):
        for sy in (1, -1):
            pairs = []
            for a in range(count_x):
                for b in range(count_y):
                    if 0 <= a + sx < count_x and 0 <= b + sy < count_y:
                        pairs.append((a * count_y + b, (a + sx) * count_y + (b + sy)))
            pieces = []
            for block, wx, wy in items:
                bx, by = block.shape[0], block.shape[1]
                x0 = bx - wx if sx == 1 else 0
                y0 = by - wy if sy == 1 else 0
                pieces.append(block[x0 : x0 + wx, y0 : y0 + wy])
            faces[(sx, sy)] = send(pieces, ("xb", "yb"), pairs)
    for index, (block, wx, wy) in enumerate(items):
        low = jnp.concatenate(
            [faces[(1, 1)][index], faces[("x", 1)][index], faces[(1, -1)][index]], axis=1
        )
        middle = jnp.concatenate(
            [faces[("y", 1)][index], block, faces[("y", -1)][index]], axis=1
        )
        high = jnp.concatenate(
            [faces[(-1, 1)][index], faces[("x", -1)][index], faces[(-1, -1)][index]], axis=1
        )
        boxes.append(jnp.concatenate([low, middle, high], axis=0))
    for index, (block, wy) in enumerate(extras):
        index += len(items)
        boxes.append(
            jnp.concatenate([faces[("y", 1)][index], block, faces[("y", -1)][index]], axis=1)
        )
    return boxes


def pad_z(box):
    return jnp.pad(box, ((0, 0), (0, 0), (1, 1)))


def trim(box):
    return box[1:-1, 1:-1, :]


def neighbours(padded):
    return [
        padded[2:, 1:-1, 1:-1],
        padded[:-2, 1:-1, 1:-1],
        padded[1:-1, 2:, 1:-1],
        padded[1:-1, :-2, 1:-1],
        padded[1:-1, 1:-1, 2:],
        padded[1:-1, 1:-1, :-2],
    ]


def apply_operator(padded, field, weights, diagonal):
    result = diagonal * field
    for weight, other in zip(weights, neighbours(padded)):
        result = result - weight * other
    return result


def pair_matrix(count):
    rows = jnp.arange(count // 2)[:, None]
    cols = jnp.arange(count)[None, :] // 2
    return (rows == cols).astype(jnp.float32)


def restrict_field(field):
    sx, sy, sz = field.shape
    halves = field.reshape(sx // 2, 2, sy, sz)
    summed = halves[:, 0] + halves[:, 1]
    summed = jnp.einsum(
        "xyZ,zZ->xyz", summed, pair_matrix(sz), precision=lax.Precision.HIGHEST
    )
    pairs_y = jnp.broadcast_to(pair_matrix(sy), (sx // 2, sy // 2, sy))
    summed = jnp.einsum(
        "xyY,xYz->xyz", pairs_y, summed, precision=lax.Precision.HIGHEST
    )
    return summed * 0.125


def box_weights(padded_coef, scale):
    centre = padded_coef[1:-1, 1:-1, 1:-1]
    outside = centre == 0.0
    weights = [
        jnp.where(outside, 0.0, 0.5 * scale * (centre + other))
        for other in neighbours(padded_coef)
    ]
    diagonal = damping_alpha + weights[0]
    for other in weights[1:]:
        diagonal = diagonal + other
    return (weights, diagonal)


def smooth_box(start, right_side, coefficient, scale):
    weights, diagonal = box_weights(pad_z(coefficient), scale)
    if start is None:
        start = jnp.zeros_like(right_side)
        residual = right_side
    else:
        residual = right_side - apply_operator(pad_z(start), trim(start), weights, diagonal)
        start = trim(start)
    first_step = residual / (cheb_theta * diagonal)
    first = start + first_step
    weights = [trim(w) for w in weights]
    diagonal = trim(diagonal)
    right_side = trim(right_side)
    residual = right_side - apply_operator(pad_z(first), trim(first), weights, diagonal)
    second_step = cheb_carry * trim(first_step) + cheb_resid * residual / diagonal
    second = trim(first) + second_step
    weights = [trim(w) for w in weights]
    diagonal = trim(diagonal)
    residual = trim(right_side) - apply_operator(pad_z(second), trim(second), weights, diagonal)
    return (trim(second), residual)


def collect_blocks(right_side, coefficient):
    count = lax.axis_size("xb") * lax.axis_size("yb")
    flat = jnp.concatenate([right_side.reshape(1, -1), coefficient.reshape(1, -1)], axis=1)
    return lax.all_to_all(
        jnp.broadcast_to(flat, (count, flat.shape[1])), ("xb", "yb"), 0, 0, tiled=True
    )


def coarse_kernel_body(scale, count_x, count_y, block_y, nz, iters):
    rows = count_x * count_y
    width = block_y * nz

    def body(mine_ref, every_ref, out_ref, field_ref):
        f = every_ref[:, :width]
        k = every_ref[:, width:]
        row = jax.lax.broadcasted_iota(jnp.int32, (rows, width), 0)
        lane = jax.lax.broadcasted_iota(jnp.int32, (rows, width), 1)
        zpos = lane % nz
        ypos = lane // nz
        ydev = row % count_y
        up_inside = ypos < block_y - 1
        down_inside = ypos > 0
        masks = [
            row < rows - count_y,
            row >= count_y,
            up_inside | (ydev < count_y - 1),
            down_inside | (ydev > 0),
            zpos < nz - 1,
            zpos > 0,
        ]

        def nbs(a):
            up = pltpu.roll(a, width - nz, 1)
            up = jnp.where(up_inside, up, pltpu.roll(up, rows - 1, 0))
            down = pltpu.roll(a, nz, 1)
            down = jnp.where(down_inside, down, pltpu.roll(down, 1, 0))
            found = [
                pltpu.roll(a, rows - count_y, 0),
                pltpu.roll(a, count_y, 0),
                up,
                down,
                pltpu.roll(a, width - 1, 1),
                pltpu.roll(a, 1, 1),
            ]
            return [jnp.where(m, other, 0.0) for m, other in zip(masks, found)]

        weights = [(0.5 * scale) * (k + other) for other in nbs(k)]
        diagonal = damping_alpha + weights[0]
        for other in weights[1:]:
            diagonal = diagonal + other

        def apply(v):
            result = diagonal * v
            for w, other in zip(weights, nbs(v)):
                result = result - w * other
            return result

        field = jnp.zeros_like(f)
        for _ in range(iters):
            field = field + jacobi_weight * (f - apply(field)) / diagonal
        leftover = f - apply(field)
        image = diagonal * jnp.ones_like(f)
        for w, m in zip(weights, masks):
            image = image - w * jnp.where(m, 1.0, 0.0)
        field_ref[...] = field + jnp.sum(leftover) / jnp.sum(image)
        out_ref[...] = field_ref[pl.ds(mine_ref[0], 1), :]

    return body


def coarse_pallas(mine, every, scale, count_x, count_y, block_y, nz, iters):
    width = every.shape[1] // 2
    return pl.pallas_call(
        coarse_kernel_body(scale, count_x, count_y, block_y, nz, iters),
        out_shape=jax.ShapeDtypeStruct((1, width), jnp.float32),
        in_specs=[
            pl.BlockSpec(memory_space=pltpu.SMEM),
            pl.BlockSpec(memory_space=pltpu.VMEM),
        ],
        out_specs=pl.BlockSpec(memory_space=pltpu.VMEM),
        scratch_shapes=[pltpu.VMEM((every.shape[0], width), jnp.float32)],
    )(mine, every)


def per_device(initial_guess, right_side, coefficient):
    mid_coef = restrict_field(coefficient)
    low_coef = restrict_field(mid_coef)
    low_size = low_coef.shape[0]
    low_first = min(3, low_size)
    assert low_first == 3 or 2 * low_size >= 3
    guess_b, rhs_b, coef_b, mid_coef_b, low_coef_b = exchange_once(
        [(initial_guess, 3, 7), (right_side, 2, 7), (coefficient, 3, 7)],
        [(mid_coef, 3), (low_coef, 3)],
    )
    fine, fine_res = smooth_box(guess_b, rhs_b[:, 1:-1], coef_b, 1.0)
    fine = fine[:, 4:-4]
    mid_rhs = restrict_field(fine_res)
    mid_rhs_b, mid_coef_b, low_coef_b = exchange(
        [(mid_rhs, 2), (mid_coef_b, 3), (low_coef_b, low_first)], "xb", 0
    )[0]
    middle, mid_res = smooth_box(None, mid_rhs_b, mid_coef_b, 0.25)
    low_rhs = restrict_field(mid_res)
    (low_rhs_b,) = exchange([(low_rhs, 3)], "yb", 1)[0]
    forwards = ()
    if low_first < 3:
        forwards = ((low_coef_b, (2 * low_size - 3, low_size), (2 * low_size, low_size + 3)),)
    (low_rhs_b,), boxes = exchange([(low_rhs_b, 2)], "xb", 0, forwards)
    if low_first < 3:
        (low_coef_b,) = boxes
    lower, low_res = smooth_box(None, low_rhs_b[:, 1:-1], low_coef_b, 0.0625)
    coarse_rhs = restrict_field(low_res)
    sx, sy, sz = coarse_rhs.shape
    assert sx == 1
    every = collect_blocks(coarse_rhs, restrict_field(low_coef))
    count_y = lax.axis_size("yb")
    mine = (lax.axis_index("xb") * count_y + lax.axis_index("yb")).astype(jnp.int32).reshape(1)
    coarse = coarse_pallas(
        mine, every, 0.015625, lax.axis_size("xb"), count_y, sy, sz, COARSE_ITERS
    ).reshape(sx, sy, sz)
    return (fine, middle, lower, coarse)


def solution(mesh):
    placed = (P("xb", "yb", None), P("xb", "yb", None), P("xb", "yb", None))
    return jax.shard_map(
        per_device,
        mesh=mesh,
        in_specs=placed,
        out_specs=(
            P("xb", "yb", None),
            P("xb", "yb", None),
            P("xb", "yb", None),
            P("xb", "yb", None),
        ),
        check_vma=False,
    )
```

```python
import jax
import jax.numpy as jnp
from jax import lax
from jax.experimental import pallas as pl
from jax.experimental.pallas import tpu as pltpu
from jax.sharding import PartitionSpec as P


COARSE_ITERS = 8


damping_alpha = 0.05
cheb_theta = 1.15
cheb_delta = 0.85
cheb_sigma = cheb_theta / cheb_delta
cheb_first = 1.0 / cheb_sigma
cheb_second = 1.0 / (2.0 * cheb_sigma - cheb_first)
cheb_carry = cheb_second * cheb_first
cheb_resid = 2.0 * cheb_second / cheb_delta
jacobi_weight = 0.8


def exchange(items, axis, dim, forwards=()):
    count = lax.axis_size(axis)
    low = [[] for _ in items]
    high = [[] for _ in items]
    boxes = [box for box, _, _ in forwards]
    reach = max(-(-width // block.shape[dim]) for block, width in items)
    for hop in range(1, reach + 1):
        for sign in (1, -1):
            pieces = []
            owners = []
            for index, (block, width) in enumerate(items):
                size = block.shape[dim]
                rows = min(size, width - (hop - 1) * size)
                if rows <= 0:
                    continue
                begin = size - rows if sign == 1 else 0
                pieces.append(lax.slice_in_dim(block, begin, begin + rows, axis=dim))
                owners.append(index)
            if hop == 1:
                for index, (box, rows_low, rows_high) in enumerate(forwards):
                    rows = rows_low if sign == 1 else rows_high
                    pieces.append(lax.slice_in_dim(box, rows[0], rows[1], axis=dim))
                    owners.append(-1 - index)
            common = [max(p.shape[d] for p in pieces) for d in (1, 2)]
            joined = jnp.concatenate(
                [
                    jnp.pad(p, ((0, 0), (0, common[0] - p.shape[1]), (0, common[1] - p.shape[2])))
                    for p in pieces
                ],
                axis=0,
            )
            if sign == 1:
                pairs = [(i, i + hop) for i in range(count - hop)]
            else:
                pairs = [(i + hop, i) for i in range(count - hop)]
            got = lax.ppermute(joined, axis, pairs)
            offset = 0
            for index, piece in zip(owners, pieces):
                part = got[offset : offset + piece.shape[0], : piece.shape[1], : piece.shape[2]]
                offset += piece.shape[0]
                if index < 0:
                    box = boxes[-1 - index]
                    parts = [part, box] if sign == 1 else [box, part]
                    boxes[-1 - index] = jnp.concatenate(parts, axis=dim)
                elif sign == 1:
                    low[index].insert(0, part)
                else:
                    high[index].append(part)
    extended = [
        jnp.concatenate(low[i] + [block] + high[i], axis=dim)
        for i, (block, width) in enumerate(items)
    ]
    return extended, boxes


def send(pieces, axis, pairs):
    common = [max(p.shape[d] for p in pieces) for d in (1, 2)]
    joined = jnp.concatenate(
        [
            jnp.pad(p, ((0, 0), (0, common[0] - p.shape[1]), (0, common[1] - p.shape[2])))
            for p in pieces
        ],
        axis=0,
    )
    got = lax.ppermute(joined, axis, pairs)
    parts = []
    offset = 0
    for piece in pieces:
        parts.append(got[offset : offset + piece.shape[0], : piece.shape[1], : piece.shape[2]])
        offset += piece.shape[0]
    return parts


def exchange_once(items, extras):
    count_x = lax.axis_size("xb")
    count_y = lax.axis_size("yb")
    boxes = []
    faces = {}
    for sign in (1, -1):
        pairs = [(i, i + 1) for i in range(count_x - 1)]
        if sign == -1:
            pairs = [(j, i) for i, j in pairs]
        pieces = []
        for block, wx, wy in items:
            size = block.shape[0]
            begin = size - wx if sign == 1 else 0
            pieces.append(block[begin : begin + wx])
        faces[("x", sign)] = send(pieces, "xb", pairs)
    for sign in (1, -1):
        pairs = [(i, i + 1) for i in range(count_y - 1)]
        if sign == -1:
            pairs = [(j, i) for i, j in pairs]
        pieces = []
        for block, _, wy in list(items) + [(b, 0, w) for b, w in extras]:
            size = block.shape[1]
            begin = size - wy if sign == 1 else 0
            pieces.append(block[:, begin : begin + wy])
        faces[("y", sign)] = send(pieces, "yb", pairs)
    for sx in (1, -1):
        for sy in (1, -1):
            pairs = []
            for a in range(count_x):
                for b in range(count_y):
                    if 0 <= a + sx < count_x and 0 <= b + sy < count_y:
                        pairs.append((a * count_y + b, (a + sx) * count_y + (b + sy)))
            pieces = []
            for block, wx, wy in items:
                cy = wy - 1
                bx, by = block.shape[0], block.shape[1]
                x0 = bx - wx if sx == 1 else 0
                y0 = by - cy if sy == 1 else 0
                pieces.append(block[x0 : x0 + wx, y0 : y0 + cy])
            faces[(sx, sy)] = send(pieces, ("xb", "yb"), pairs)
    for index, (block, wx, wy) in enumerate(items):
        for sx in (1, -1):
            faces[(sx, 1)][index] = jnp.pad(faces[(sx, 1)][index], ((0, 0), (1, 0), (0, 0)))
            faces[(sx, -1)][index] = jnp.pad(faces[(sx, -1)][index], ((0, 0), (0, 1), (0, 0)))
        low = jnp.concatenate(
            [faces[(1, 1)][index], faces[("x", 1)][index], faces[(1, -1)][index]], axis=1
        )
        middle = jnp.concatenate(
            [faces[("y", 1)][index], block, faces[("y", -1)][index]], axis=1
        )
        high = jnp.concatenate(
            [faces[(-1, 1)][index], faces[("x", -1)][index], faces[(-1, -1)][index]], axis=1
        )
        boxes.append(jnp.concatenate([low, middle, high], axis=0))
    for index, (block, wy) in enumerate(extras):
        index += len(items)
        boxes.append(
            jnp.concatenate([faces[("y", 1)][index], block, faces[("y", -1)][index]], axis=1)
        )
    return boxes


def pad_z(box):
    return jnp.pad(box, ((0, 0), (0, 0), (1, 1)))


def trim(box):
    return box[1:-1, 1:-1, :]


def neighbours(padded):
    return [
        padded[2:, 1:-1, 1:-1],
        padded[:-2, 1:-1, 1:-1],
        padded[1:-1, 2:, 1:-1],
        padded[1:-1, :-2, 1:-1],
        padded[1:-1, 1:-1, 2:],
        padded[1:-1, 1:-1, :-2],
    ]


def apply_operator(padded, field, weights, diagonal):
    result = diagonal * field
    for weight, other in zip(weights, neighbours(padded)):
        result = result - weight * other
    return result


def pair_matrix(count):
    rows = jnp.arange(count // 2)[:, None]
    cols = jnp.arange(count)[None, :] // 2
    return (rows == cols).astype(jnp.float32)


def restrict_field(field):
    sx, sy, sz = field.shape
    halves = field.reshape(sx // 2, 2, sy, sz)
    summed = halves[:, 0] + halves[:, 1]
    summed = jnp.einsum(
        "xyZ,zZ->xyz", summed, pair_matrix(sz), precision=lax.Precision.HIGHEST
    )
    pairs_y = jnp.broadcast_to(pair_matrix(sy), (sx // 2, sy // 2, sy))
    summed = jnp.einsum(
        "xyY,xYz->xyz", pairs_y, summed, precision=lax.Precision.HIGHEST
    )
    return summed * 0.125


def box_weights(padded_coef, scale):
    centre = padded_coef[1:-1, 1:-1, 1:-1]
    outside = centre == 0.0
    weights = [
        jnp.where(outside, 0.0, 0.5 * scale * (centre + other))
        for other in neighbours(padded_coef)
    ]
    diagonal = damping_alpha + weights[0]
    for other in weights[1:]:
        diagonal = diagonal + other
    return (weights, diagonal)


def smooth_box(start, right_side, coefficient, scale):
    weights, diagonal = box_weights(pad_z(coefficient), scale)
    if start is None:
        start = jnp.zeros_like(right_side)
        residual = right_side
    else:
        residual = right_side - apply_operator(pad_z(start), trim(start), weights, diagonal)
        start = trim(start)
    first_step = residual / (cheb_theta * diagonal)
    first = start + first_step
    weights = [trim(w) for w in weights]
    diagonal = trim(diagonal)
    right_side = trim(right_side)
    residual = right_side - apply_operator(pad_z(first), trim(first), weights, diagonal)
    second_step = cheb_carry * trim(first_step) + cheb_resid * residual / diagonal
    second = trim(first) + second_step
    weights = [trim(w) for w in weights]
    diagonal = trim(diagonal)
    residual = trim(right_side) - apply_operator(pad_z(second), trim(second), weights, diagonal)
    return (trim(second), residual)


def collect_blocks(right_side, coefficient):
    count = lax.axis_size("xb") * lax.axis_size("yb")
    flat = jnp.concatenate([right_side.reshape(1, -1), coefficient.reshape(1, -1)], axis=1)
    return lax.all_to_all(
        jnp.broadcast_to(flat, (count, flat.shape[1])), ("xb", "yb"), 0, 0, tiled=True
    )


def coarse_kernel_body(scale, count_x, count_y, block_y, nz, iters):
    rows = count_x * count_y
    width = block_y * nz

    def body(every_ref, out_ref):
        f = every_ref[:, :width]
        k = every_ref[:, width:]
        row = jax.lax.broadcasted_iota(jnp.int32, (rows, width), 0)
        lane = jax.lax.broadcasted_iota(jnp.int32, (rows, width), 1)
        zpos = lane % nz
        ypos = lane // nz
        ydev = row % count_y
        up_inside = ypos < block_y - 1
        down_inside = ypos > 0
        masks = [
            row < rows - count_y,
            row >= count_y,
            up_inside | (ydev < count_y - 1),
            down_inside | (ydev > 0),
            zpos < nz - 1,
            zpos > 0,
        ]

        def nbs(a):
            up = pltpu.roll(a, width - nz, 1)
            up = jnp.where(up_inside, up, pltpu.roll(up, rows - 1, 0))
            down = pltpu.roll(a, nz, 1)
            down = jnp.where(down_inside, down, pltpu.roll(down, 1, 0))
            found = [
                pltpu.roll(a, rows - count_y, 0),
                pltpu.roll(a, count_y, 0),
                up,
                down,
                pltpu.roll(a, width - 1, 1),
                pltpu.roll(a, 1, 1),
            ]
            return [jnp.where(m, other, 0.0) for m, other in zip(masks, found)]

        weights = [(0.5 * scale) * (k + other) for other in nbs(k)]
        diagonal = damping_alpha + weights[0]
        for other in weights[1:]:
            diagonal = diagonal + other

        def apply(v):
            result = diagonal * v
            for w, other in zip(weights, nbs(v)):
                result = result - w * other
            return result

        field = jnp.zeros_like(f)
        for _ in range(iters):
            field = field + jacobi_weight * (f - apply(field)) / diagonal
        leftover = f - apply(field)
        image = diagonal * jnp.ones_like(f)
        for w, m in zip(weights, masks):
            image = image - w * jnp.where(m, 1.0, 0.0)
        out_ref[...] = field + jnp.sum(leftover) / jnp.sum(image)

    return body


def coarse_pallas(every, scale, count_x, count_y, block_y, nz, iters):
    return pl.pallas_call(
        coarse_kernel_body(scale, count_x, count_y, block_y, nz, iters),
        out_shape=jax.ShapeDtypeStruct((every.shape[0], every.shape[1] // 2), jnp.float32),
    )(every)


def per_device(initial_guess, right_side, coefficient):
    mid_coef = restrict_field(coefficient)
    low_coef = restrict_field(mid_coef)
    low_size = low_coef.shape[0]
    low_first = min(3, low_size)
    assert low_first == 3 or 2 * low_size >= 3
    guess_b, rhs_b, coef_b, mid_coef_b, low_coef_b = exchange_once(
        [(initial_guess, 3, 7), (right_side, 2, 7), (coefficient, 3, 7)],
        [(mid_coef, 3), (low_coef, 3)],
    )
    fine, fine_res = smooth_box(guess_b, rhs_b[:, 1:-1], coef_b, 1.0)
    fine = fine[:, 4:-4]
    mid_rhs = restrict_field(fine_res)
    mid_rhs_b, mid_coef_b, low_coef_b = exchange(
        [(mid_rhs, 2), (mid_coef_b, 3), (low_coef_b, low_first)], "xb", 0
    )[0]
    middle, mid_res = smooth_box(None, mid_rhs_b, mid_coef_b, 0.25)
    low_rhs = restrict_field(mid_res)
    (low_rhs_b,) = exchange([(low_rhs, 3)], "yb", 1)[0]
    forwards = ()
    if low_first < 3:
        forwards = ((low_coef_b, (2 * low_size - 3, low_size), (2 * low_size, low_size + 3)),)
    (low_rhs_b,), boxes = exchange([(low_rhs_b, 2)], "xb", 0, forwards)
    if low_first < 3:
        (low_coef_b,) = boxes
    lower, low_res = smooth_box(None, low_rhs_b[:, 1:-1], low_coef_b, 0.0625)
    coarse_rhs = restrict_field(low_res)
    sx, sy, sz = coarse_rhs.shape
    assert sx == 1
    every = collect_blocks(coarse_rhs, restrict_field(low_coef))
    count_y = lax.axis_size("yb")
    coarse_all = coarse_pallas(every, 0.015625, lax.axis_size("xb"), count_y, sy, sz, COARSE_ITERS)
    mine = lax.axis_index("xb") * count_y + lax.axis_index("yb")
    coarse = lax.dynamic_slice_in_dim(coarse_all, mine, 1, axis=0).reshape(sx, sy, sz)
    return (fine, middle, lower, coarse)


def solution(mesh):
    placed = (P("xb", "yb", None), P("xb", "yb", None), P("xb", "yb", None))
    return jax.shard_map(
        per_device,
        mesh=mesh,
        in_specs=placed,
        out_specs=(
            P("xb", "yb", None),
            P("xb", "yb", None),
            P("xb", "yb", None),
            P("xb", "yb", None),
        ),
        check_vma=False,
    )
```

```python
import jax
import jax.numpy as jnp
from jax import lax
from jax.experimental import pallas as pl
from jax.experimental.pallas import tpu as pltpu
from jax.sharding import PartitionSpec as P


COARSE_ITERS = 8


damping_alpha = 0.05
cheb_theta = 1.15
cheb_delta = 0.85
cheb_sigma = cheb_theta / cheb_delta
cheb_first = 1.0 / cheb_sigma
cheb_second = 1.0 / (2.0 * cheb_sigma - cheb_first)
cheb_carry = cheb_second * cheb_first
cheb_resid = 2.0 * cheb_second / cheb_delta
jacobi_weight = 0.8


def exchange(items, axis, dim, forwards=()):
    count = lax.axis_size(axis)
    low = [[] for _ in items]
    high = [[] for _ in items]
    boxes = [box for box, _, _ in forwards]
    reach = max(-(-width // block.shape[dim]) for block, width in items)
    for hop in range(1, reach + 1):
        for sign in (1, -1):
            pieces = []
            owners = []
            for index, (block, width) in enumerate(items):
                size = block.shape[dim]
                rows = min(size, width - (hop - 1) * size)
                if rows <= 0:
                    continue
                begin = size - rows if sign == 1 else 0
                pieces.append(lax.slice_in_dim(block, begin, begin + rows, axis=dim))
                owners.append(index)
            if hop == 1:
                for index, (box, rows_low, rows_high) in enumerate(forwards):
                    rows = rows_low if sign == 1 else rows_high
                    pieces.append(lax.slice_in_dim(box, rows[0], rows[1], axis=dim))
                    owners.append(-1 - index)
            common = [max(p.shape[d] for p in pieces) for d in (1, 2)]
            joined = jnp.concatenate(
                [
                    jnp.pad(p, ((0, 0), (0, common[0] - p.shape[1]), (0, common[1] - p.shape[2])))
                    for p in pieces
                ],
                axis=0,
            )
            if sign == 1:
                pairs = [(i, i + hop) for i in range(count - hop)]
            else:
                pairs = [(i + hop, i) for i in range(count - hop)]
            got = lax.ppermute(joined, axis, pairs)
            offset = 0
            for index, piece in zip(owners, pieces):
                part = got[offset : offset + piece.shape[0], : piece.shape[1], : piece.shape[2]]
                offset += piece.shape[0]
                if index < 0:
                    box = boxes[-1 - index]
                    parts = [part, box] if sign == 1 else [box, part]
                    boxes[-1 - index] = jnp.concatenate(parts, axis=dim)
                elif sign == 1:
                    low[index].insert(0, part)
                else:
                    high[index].append(part)
    extended = [
        jnp.concatenate(low[i] + [block] + high[i], axis=dim)
        for i, (block, width) in enumerate(items)
    ]
    return extended, boxes


def send(pieces, axis, pairs):
    common = [max(p.shape[d] for p in pieces) for d in (1, 2)]
    joined = jnp.concatenate(
        [
            jnp.pad(p, ((0, 0), (0, common[0] - p.shape[1]), (0, common[1] - p.shape[2])))
            for p in pieces
        ],
        axis=0,
    )
    got = lax.ppermute(joined, axis, pairs)
    parts = []
    offset = 0
    for piece in pieces:
        parts.append(got[offset : offset + piece.shape[0], : piece.shape[1], : piece.shape[2]])
        offset += piece.shape[0]
    return parts


def exchange_once(items, extras):
    count_x = lax.axis_size("xb")
    count_y = lax.axis_size("yb")
    boxes = []
    faces = {}
    for sign in (1, -1):
        pairs = [(i, i + 1) for i in range(count_x - 1)]
        if sign == -1:
            pairs = [(j, i) for i, j in pairs]
        pieces = []
        for block, wx, wy in items:
            size = block.shape[0]
            begin = size - wx if sign == 1 else 0
            pieces.append(block[begin : begin + wx])
        faces[("x", sign)] = send(pieces, "xb", pairs)
    for sign in (1, -1):
        pairs = [(i, i + 1) for i in range(count_y - 1)]
        if sign == -1:
            pairs = [(j, i) for i, j in pairs]
        pieces = []
        for block, _, wy in list(items) + [(b, 0, w) for b, w in extras]:
            size = block.shape[1]
            begin = size - wy if sign == 1 else 0
            pieces.append(block[:, begin : begin + wy])
        faces[("y", sign)] = send(pieces, "yb", pairs)
    for sx in (1, -1):
        for sy in (1, -1):
            pairs = []
            for a in range(count_x):
                for b in range(count_y):
                    if 0 <= a + sx < count_x and 0 <= b + sy < count_y:
                        pairs.append((a * count_y + b, (a + sx) * count_y + (b + sy)))
            pieces = []
            for block, wx, wy in items:
                bx, by = block.shape[0], block.shape[1]
                x0 = bx - wx if sx == 1 else 0
                y0 = by - wy if sy == 1 else 0
                pieces.append(block[x0 : x0 + wx, y0 : y0 + wy])
            faces[(sx, sy)] = send(pieces, ("xb", "yb"), pairs)
    for index, (block, wx, wy) in enumerate(items):
        low = jnp.concatenate(
            [faces[(1, 1)][index], faces[("x", 1)][index], faces[(1, -1)][index]], axis=1
        )
        middle = jnp.concatenate(
            [faces[("y", 1)][index], block, faces[("y", -1)][index]], axis=1
        )
        high = jnp.concatenate(
            [faces[(-1, 1)][index], faces[("x", -1)][index], faces[(-1, -1)][index]], axis=1
        )
        boxes.append(jnp.concatenate([low, middle, high], axis=0))
    for index, (block, wy) in enumerate(extras):
        index += len(items)
        boxes.append(
            jnp.concatenate([faces[("y", 1)][index], block, faces[("y", -1)][index]], axis=1)
        )
    return boxes


def pad_z(box):
    return jnp.pad(box, ((0, 0), (0, 0), (1, 1)))


def trim(box):
    return box[1:-1, 1:-1, :]


def neighbours(padded):
    return [
        padded[2:, 1:-1, 1:-1],
        padded[:-2, 1:-1, 1:-1],
        padded[1:-1, 2:, 1:-1],
        padded[1:-1, :-2, 1:-1],
        padded[1:-1, 1:-1, 2:],
        padded[1:-1, 1:-1, :-2],
    ]


def apply_operator(padded, field, weights, diagonal):
    result = diagonal * field
    for weight, other in zip(weights, neighbours(padded)):
        result = result - weight * other
    return result


def pair_matrix(count):
    rows = jnp.arange(count // 2)[:, None]
    cols = jnp.arange(count)[None, :] // 2
    return (rows == cols).astype(jnp.float32)


def restrict_field(field):
    sx, sy, sz = field.shape
    halves = field.reshape(sx // 2, 2, sy, sz)
    summed = halves[:, 0] + halves[:, 1]
    summed = jnp.einsum(
        "xyZ,zZ->xyz", summed, pair_matrix(sz), precision=lax.Precision.HIGHEST
    )
    pairs_y = jnp.broadcast_to(pair_matrix(sy), (sx // 2, sy // 2, sy))
    summed = jnp.einsum(
        "xyY,xYz->xyz", pairs_y, summed, precision=lax.Precision.HIGHEST
    )
    return summed * 0.125


def box_weights(padded_coef, scale):
    centre = padded_coef[1:-1, 1:-1, 1:-1]
    outside = centre == 0.0
    weights = [
        jnp.where(outside, 0.0, 0.5 * scale * (centre + other))
        for other in neighbours(padded_coef)
    ]
    diagonal = damping_alpha + weights[0]
    for other in weights[1:]:
        diagonal = diagonal + other
    return (weights, diagonal)


def smooth_box(start, right_side, coefficient, scale):
    weights, diagonal = box_weights(pad_z(coefficient), scale)
    if start is None:
        start = jnp.zeros_like(right_side)
        residual = right_side
    else:
        residual = right_side - apply_operator(pad_z(start), trim(start), weights, diagonal)
        start = trim(start)
    first_step = residual / (cheb_theta * diagonal)
    first = start + first_step
    weights = [trim(w) for w in weights]
    diagonal = trim(diagonal)
    right_side = trim(right_side)
    residual = right_side - apply_operator(pad_z(first), trim(first), weights, diagonal)
    second_step = cheb_carry * trim(first_step) + cheb_resid * residual / diagonal
    second = trim(first) + second_step
    weights = [trim(w) for w in weights]
    diagonal = trim(diagonal)
    residual = trim(right_side) - apply_operator(pad_z(second), trim(second), weights, diagonal)
    return (trim(second), residual)


def collect_blocks(right_side, coefficient):
    count = lax.axis_size("xb") * lax.axis_size("yb")
    flat = jnp.concatenate([right_side.reshape(1, -1), coefficient.reshape(1, -1)], axis=1)
    return lax.all_to_all(
        jnp.broadcast_to(flat, (count, flat.shape[1])), ("xb", "yb"), 0, 0, tiled=True
    )


def coarse_kernel_body(scale, count_x, count_y, block_y, nz, iters):
    rows = count_x * count_y
    width = block_y * nz

    def body(every_ref, out_ref):
        f = every_ref[:, :width]
        k = every_ref[:, width:]
        row = jax.lax.broadcasted_iota(jnp.int32, (rows, width), 0)
        lane = jax.lax.broadcasted_iota(jnp.int32, (rows, width), 1)
        zpos = lane % nz
        ypos = lane // nz
        ydev = row % count_y
        up_inside = ypos < block_y - 1
        down_inside = ypos > 0
        masks = [
            row < rows - count_y,
            row >= count_y,
            up_inside | (ydev < count_y - 1),
            down_inside | (ydev > 0),
            zpos < nz - 1,
            zpos > 0,
        ]

        def nbs(a):
            up = pltpu.roll(a, width - nz, 1)
            up = jnp.where(up_inside, up, pltpu.roll(up, rows - 1, 0))
            down = pltpu.roll(a, nz, 1)
            down = jnp.where(down_inside, down, pltpu.roll(down, 1, 0))
            found = [
                pltpu.roll(a, rows - count_y, 0),
                pltpu.roll(a, count_y, 0),
                up,
                down,
                pltpu.roll(a, width - 1, 1),
                pltpu.roll(a, 1, 1),
            ]
            return [jnp.where(m, other, 0.0) for m, other in zip(masks, found)]

        weights = [(0.5 * scale) * (k + other) for other in nbs(k)]
        diagonal = damping_alpha + weights[0]
        for other in weights[1:]:
            diagonal = diagonal + other

        def apply(v):
            result = diagonal * v
            for w, other in zip(weights, nbs(v)):
                result = result - w * other
            return result

        field = jnp.zeros_like(f)
        for _ in range(iters):
            field = field + jacobi_weight * (f - apply(field)) / diagonal
        leftover = f - apply(field)
        image = diagonal * jnp.ones_like(f)
        for w, m in zip(weights, masks):
            image = image - w * jnp.where(m, 1.0, 0.0)
        out_ref[...] = field + jnp.sum(leftover) / jnp.sum(image)

    return body


def coarse_pallas(every, scale, count_x, count_y, block_y, nz, iters):
    return pl.pallas_call(
        coarse_kernel_body(scale, count_x, count_y, block_y, nz, iters),
        out_shape=jax.ShapeDtypeStruct((every.shape[0], every.shape[1] // 2), jnp.float32),
        compiler_params=pltpu.CompilerParams(allow_input_fusion=[True]),
    )(every)


def per_device(initial_guess, right_side, coefficient):
    mid_coef = restrict_field(coefficient)
    low_coef = restrict_field(mid_coef)
    low_size = low_coef.shape[0]
    low_first = min(3, low_size)
    assert low_first == 3 or 2 * low_size >= 3
    guess_b, rhs_b, coef_b, mid_coef_b, low_coef_b = exchange_once(
        [(initial_guess, 3, 7), (right_side, 2, 7), (coefficient, 3, 7)],
        [(mid_coef, 3), (low_coef, 3)],
    )
    fine, fine_res = smooth_box(guess_b, rhs_b[:, 1:-1], coef_b, 1.0)
    fine = fine[:, 4:-4]
    mid_rhs = restrict_field(fine_res)
    mid_rhs_b, mid_coef_b, low_coef_b = exchange(
        [(mid_rhs, 2), (mid_coef_b, 3), (low_coef_b, low_first)], "xb", 0
    )[0]
    middle, mid_res = smooth_box(None, mid_rhs_b, mid_coef_b, 0.25)
    low_rhs = restrict_field(mid_res)
    (low_rhs_b,) = exchange([(low_rhs, 3)], "yb", 1)[0]
    forwards = ()
    if low_first < 3:
        forwards = ((low_coef_b, (2 * low_size - 3, low_size), (2 * low_size, low_size + 3)),)
    (low_rhs_b,), boxes = exchange([(low_rhs_b, 2)], "xb", 0, forwards)
    if low_first < 3:
        (low_coef_b,) = boxes
    lower, low_res = smooth_box(None, low_rhs_b[:, 1:-1], low_coef_b, 0.0625)
    coarse_rhs = restrict_field(low_res)
    sx, sy, sz = coarse_rhs.shape
    assert sx == 1
    every = collect_blocks(coarse_rhs, restrict_field(low_coef))
    count_y = lax.axis_size("yb")
    coarse_all = coarse_pallas(every, 0.015625, lax.axis_size("xb"), count_y, sy, sz, COARSE_ITERS)
    mine = lax.axis_index("xb") * count_y + lax.axis_index("yb")
    coarse = lax.dynamic_slice_in_dim(coarse_all, mine, 1, axis=0).reshape(sx, sy, sz)
    return (fine, middle, lower, coarse)


def solution(mesh):
    placed = (P("xb", "yb", None), P("xb", "yb", None), P("xb", "yb", None))
    return jax.shard_map(
        per_device,
        mesh=mesh,
        in_specs=placed,
        out_specs=(
            P("xb", "yb", None),
            P("xb", "yb", None),
            P("xb", "yb", None),
            P("xb", "yb", None),
        ),
        check_vma=False,
    )
```
